512 devices in a mesh: kv: 16 (over z, core), ep: 32 (over x, y).
Axes of the slice: x: 4, y: 8, z: 8, core: 2. Of those that a mesh axis runs over, the one named last changes fastest.
Arguments:
- queries: bfloat16 [32, 64, 2048], P('ep'), may hold values from -12 to 12
- new_keys: bfloat16 [32, 64, 512], P('ep'), may hold values from -12 to 12
- new_values: bfloat16 [32, 64, 512], P('ep'), may hold values from -6 to 6
- cache_keys: bfloat16 [32, 64, 128, 512], P('ep', 'kv'), may hold values from -12 to 12
- cache_values: bfloat16 [32, 64, 128, 512], P('ep', 'kv'), may hold values from -10 to 10
- page_table: int32 [32, 64], P('ep'), may hold values from 0 to 63, each once within a row
- cached_len: int32 [32], P('ep'), may hold values from 1 to 8192, 65536 in all
- moe_rows: bfloat16 [1024, 4096], P('ep'), may hold values from -6 to 6
- expert_ids: int32 [1024, 2], P('ep'), may hold values from 0 to 7, all different within a row; in each aligned block of 32 rows (0 to 31, 32 to 63, ...) at most 16 rows name the same one
- gate_probs: float32 [1024, 2], P('ep'), may hold values from 0.1 to 0.9
- w_gate: bfloat16 [32, 4096, 2048], P('ep', None, 'kv'), may hold values from -0.09375 to 0.09375
- w_up: bfloat16 [32, 4096, 2048], P('ep', None, 'kv'), may hold values from -0.09375 to 0.09375
- w_down: bfloat16 [32, 2048, 4096], P('ep', 'kv'), may hold values from -0.09375 to 0.09375
Outputs:
- attn_out: bfloat16 [32, 64, 2048], P('ep')
- moe_out: bfloat16 [1024, 4096], P('ep', 'kv')
The draws below stay inside these ranges and needn't reach their ends.
Inputs may be any that keep to these rules, and one draw needn't show every extreme that they name: `page_table`: each row is a permutation of the 64 slots of its request. `cached_len`: cached positions at or past a request's length hold no data. `expert_ids`: each row names 2 different experts; among the 32 rows of one ep index no expert is named more than 16 times, and this bound is reached.
All inputs are finite; a program needn't handle non-finite values. No bound on the sum of `cached_len` on one device may be relied on, other than what follows from the above.
Results may differ from the reference program's by a relative error of at most 0.0085.
Values may be sent and summed in bfloat16 or wider, within the bound.
No kernel may reach another device: no remote copies, remote signals or barrier semaphores. Data moves between devices by JAX's collectives and lax.ppermute only.
A program may use at most 128 MiB of HBM per device.

```python
import math
import jax
import jax.numpy as jnp
import numpy as np
from jax import lax

D = 4096
HD = 128
EXPERTS = 8
TOP = 2
HQ = 16
KVH = 4
FF = 8192
PAGE = 128
NEW = 64
TOK_EP = 32
REQS = 32
POOL_COL = 64
MAXLEN = 8192
MTOK = 1024
CAP = 16
GROUP = 4
FF_COL = 2048
N_EP = 32


def draw_queries(key, part):
    full_shape = (REQS, NEW, HQ, HD)
    drawn = jax.random.normal(key, full_shape, jnp.float32)
    return jnp.clip(drawn, -12.0, 12.0).reshape(REQS, NEW, HQ * HD).astype(jnp.bfloat16)


def draw_new_keys(key, part):
    full_shape = (REQS, NEW, KVH, HD)
    drawn = jax.random.normal(key, full_shape, jnp.float32)
    return jnp.clip(drawn, -12.0, 12.0).reshape(REQS, NEW, KVH * HD).astype(jnp.bfloat16)


def draw_cache_keys(key, part):
    full_shape = (REQS, POOL_COL, PAGE, KVH, HD)
    drawn = jnp.clip(jax.random.normal(key, full_shape, jnp.float32), -6.0, 6.0)
    return jnp.clip(drawn, -12.0, 12.0).reshape(REQS, POOL_COL, PAGE, KVH * HD).astype(jnp.bfloat16)


def draw_cache_values(key, part):
    noise_key, page_key = jax.random.split(key)
    full_shape = (REQS, POOL_COL, PAGE, KVH * HD)
    page_shape = (REQS, POOL_COL, 1, KVH * HD)
    drawn = jax.random.normal(noise_key, full_shape, jnp.float32)
    offsets = 1.5 * jax.random.normal(page_key, page_shape, jnp.float32)
    return jnp.clip(drawn + offsets, -10.0, 10.0).astype(jnp.bfloat16)


def with_spikes(array, stream_key, source, target, shards_of, factor):
    owner, partner = [(jnp.arange(array.shape[dim]) // (array.shape[dim] // shards_of)).reshape([-1 if axis == dim else 1 for axis in range(array.ndim)]) for dim in (source, target)]
    chosen = jax.random.permutation(stream_key, shards_of)[partner]
    strong = (owner == chosen) | (owner == (partner + shards_of // 2) % shards_of)
    return jnp.where(strong, factor * array, array)


def shard_levels(rng, dims, cuts, smallest, top_value):
    factor_of = 1.0
    for axis_at, shards_of in cuts:
        draws = jax.random.uniform(jax.random.fold_in(jax.random.fold_in(rng, 6), axis_at), (shards_of,), jnp.float32, smallest / len(cuts), top_value / len(cuts))
        factor_of = factor_of * jnp.repeat(jnp.exp(draws), dims[axis_at] // shards_of).reshape((-1,) + (1,) * (len(dims) - 1 - axis_at))
    return factor_of


def split_up(count, total, reach, slope):
    portions = [(1 << 20) // math.isqrt(standing ** slope) + 1 for standing in range(2, count + 1)]
    rest, holding = total - reach - (count - 1), [1] * (count - 1)
    while rest > 0:
        candidates = [i for i in range(count - 1) if holding[i] < reach]
        pool, left = sum([portions[i] for i in candidates]), rest
        for i in candidates:
            addition = min(reach - holding[i], max(1, left * portions[i] // pool), rest)
            holding[i] = holding[i] + addition
            rest = rest - addition
    return np.array([reach] + holding)


def ragged_sizes(stream_key, amount, total, most, slope):
    if amount == 2:
        one = jax.random.randint(stream_key, (), max(1, total - most), min(most, total - 1) + 1)
        return jnp.stack([one, total - one])
    tallies = jnp.asarray(split_up(amount, total, most, slope), jnp.int32)
    pairs = (amount - 1) // 2
    giver, sink = tallies[1:1 + 2 * pairs:2], tallies[2:2 + 2 * pairs:2]
    margin = jnp.minimum(giver - 1, most - sink)
    shifted = jax.random.randint(jax.random.fold_in(stream_key, 1), (pairs,), 0, 1 << 20) % (margin + 1)
    tallies = tallies.at[1:1 + 2 * pairs:2].set(giver - shifted).at[2:2 + 2 * pairs:2].set(sink + shifted)
    return tallies[jax.random.permutation(jax.random.fold_in(stream_key, 2), amount)]


def routed_block(own_key, own, number, rows, count, top, limit, lean):
    sequence = jax.random.permutation(own_key, count)
    heavy_load, common = portions_of(count, rows * top, limit, lean, True), portions_of(count, rows * top, limit, lean, False)
    places = jnp.arange(count)

    def named(tallies, offset_by):
        used = int((tallies > 0).sum())
        fixed = max(1, used // 4)
        passed = fixed + (places - fixed + offset_by * (used - fixed)) % max(1, count - fixed)
        return jnp.zeros((count,), jnp.int32).at[sequence[jnp.where(places < fixed, places, passed)]].set(jnp.asarray(tallies, jnp.int32))

    tallies = jnp.where(number % 4 == 0, named(heavy_load, number // 4), named(common, number - number // 4 - 1))
    mixed = jax.random.permutation(jax.random.fold_in(own, 3), count)
    source_of, sink = mixed[0:count // 2 * 2:2], mixed[1:count // 2 * 2:2]
    room = jnp.minimum(tallies[source_of] - 1, limit - tallies[sink]) // 2
    room = jnp.where((source_of == sequence[0]) | (sink == sequence[0]) | (tallies[sink] == 0), 0, jnp.maximum(room, 0))
    passed = jax.random.randint(jax.random.fold_in(own, 4), (count // 2,), 0, 1 << 20) % (room + 1)
    tallies = tallies.at[source_of].add(-passed).at[sink].add(passed)
    labels = jnp.searchsorted(jnp.cumsum(tallies), jnp.arange(rows * top), side="right").astype(jnp.int32)
    grid = labels.reshape(top, rows).T
    grid = grid[jax.random.permutation(jax.random.fold_in(own, 1), rows)]
    offset_by = jax.random.randint(jax.random.fold_in(own, 2), (rows, 1), 0, top)
    return jnp.take_along_axis(grid, (jnp.arange(top)[None, :] + offset_by) % top, axis=1)


def portions_of(count, total, bound, slope, full):
    loads = [(1 << 20) // math.isqrt(rank ** slope) + 1 for rank in range(1, count + 1)]
    largest = bound if full else min(bound, max(-(-total // count), total * loads[0] // sum(loads)))
    least = 1 if total - largest >= count - 1 else 0
    given, rest = [largest] + [least] * (count - 1), total - largest - least * (count - 1)
    while rest > 0:
        candidates = [i for i in range(1, count) if given[i] < largest] or [i for i in range(1, count) if given[i] < bound]
        whole, budget = sum([loads[i] for i in candidates]), rest
        for i in candidates:
            extra = min(bound - given[i], max(1, budget * loads[i] // whole), rest)
            given[i] = given[i] + extra
            rest = rest - extra
    return np.array(given)


def scatter_about(key, shape, spread, limit, pieces=(), kind=jnp.bfloat16):
    array = jax.random.normal(key, shape, jnp.float32) * spread
    if len(pieces) > 0:
        array = shard_levels(key, shape, pieces, -0.22, 0.18) * array
    return jnp.clip(array, min=-limit, max=limit).astype(kind)


def gaussian_with(rng, dims, scale, limit, cuts, heavy, held_as=jnp.bfloat16):
    result = scale * jax.random.normal(rng, dims, jnp.float32)
    if cuts:
        result = result * shard_levels(rng, dims, cuts, -0.22, 0.18)
    return jnp.clip(with_spikes(result, jax.random.fold_in(rng, 3), *heavy), -limit, limit).astype(held_as)


def setup_inputs(seed: int = 0) -> dict:
    splits = jax.random.split(jax.random.key(seed), 14)
    queries = draw_queries(jax.random.fold_in(splits[13], 71), 0)
    new_keys = draw_new_keys(jax.random.fold_in(splits[13], 71), 0)
    new_values = scatter_about(splits[2], (REQS, NEW, KVH * HD), 1.0, 6.0, ((0, 32),))
    cache_keys = draw_cache_keys(jax.random.fold_in(splits[13], 71), 0)
    cache_values = draw_cache_values(jax.random.fold_in(splits[13], 71), 0)
    page_table = jax.vmap(lambda own: jax.random.permutation(own, POOL_COL))(jax.random.split(splits[5], REQS)).reshape((REQS, POOL_COL)).astype(jnp.int32)
    cached_len = ragged_sizes(splits[6], REQS, REQS * MAXLEN // 4, MAXLEN, 2).astype(jnp.int32)
    moe_rows = scatter_about(splits[7], (MTOK, D), 1.0, 6.0, ((0, 32),))
    expert_ids_keys = jax.random.split(jax.random.fold_in(splits[8], 1), MTOK // TOK_EP)
    expert_ids_turns = jax.random.permutation(jax.random.fold_in(splits[8], 3), MTOK // TOK_EP)
    expert_ids = jax.vmap(lambda own, number: routed_block(jax.random.fold_in(splits[8], 2), own, number, TOK_EP, EXPERTS, TOP, CAP, 2))(expert_ids_keys, expert_ids_turns).reshape((MTOK, TOP))
    gate_probs = jnp.clip(0.1 + 0.79999997 * jax.random.uniform(splits[9], (MTOK, TOP), jnp.float32) ** shard_levels(splits[9], (MTOK, TOP), ((0, 32),), -0.2, 0.2), 0.1, 0.9)
    w_gate = scatter_about(splits[10], (N_EP, D, FF_COL), D ** -0.5, 0.09375, ((0, 32), (2, 16)))
    w_up = scatter_about(splits[11], (N_EP, D, FF_COL), D ** -0.5, 0.09375, ((0, 32), (2, 16)))
    w_down = gaussian_with(splits[12], (N_EP, FF_COL, D), FF ** -0.5, 0.09375, ((0, 32), (1, 16)), (1, 2, 16, 2.0))
    return {"queries": queries, "new_keys": new_keys, "new_values": new_values, "cache_keys": cache_keys, "cache_values": cache_values, "page_table": page_table, "cached_len": cached_len, "moe_rows": moe_rows, "expert_ids": expert_ids, "gate_probs": gate_probs, "w_gate": w_gate, "w_up": w_up, "w_down": w_down}


ROPE_BASE = 10000.0
MASKED = -1e+30

def rotary(values, positions):
    half_width = values.shape[-1] // 2
    indices = jnp.arange(half_width, dtype=jnp.float32)
    frequency = jnp.power(ROPE_BASE, -2.0 * indices / values.shape[-1])
    angles = positions.astype(jnp.float32)[:, None] * frequency[None, :]
    cosine = jnp.cos(angles)[:, None, :]
    sine_part = jnp.sin(angles)[:, None, :]
    lower_half = values[..., :half_width]
    upper_half = values[..., half_width:]
    return jnp.concatenate([lower_half * cosine - upper_half * sine_part, upper_half * cosine + lower_half * sine_part], axis=-1)

def attend_request(queries, new_keys, new_values, cache_keys, cache_values, page_row, length):
    group_size = HQ // KVH
    positions = length + jnp.arange(NEW, dtype=jnp.int32)
    q_rot = rotary(queries.astype(jnp.float32).reshape(NEW, HQ, HD), positions).astype(jnp.bfloat16)
    k_rot = rotary(new_keys.astype(jnp.float32).reshape(NEW, KVH, HD), positions).astype(jnp.bfloat16)
    cached_k = cache_keys[page_row].reshape(POOL_COL * PAGE, KVH, HD)
    cached_v = cache_values[page_row].reshape(POOL_COL * PAGE, KVH, HD)
    all_keys = jnp.concatenate([cached_k, k_rot], axis=0).astype(jnp.float32)
    all_values = jnp.concatenate([cached_v, new_values.reshape(NEW, KVH, HD)], axis=0).astype(jnp.float32)
    cache_live = jnp.arange(POOL_COL * PAGE, dtype=jnp.int32) < length
    causal = jnp.arange(NEW, dtype=jnp.int32)[None, :] <= jnp.arange(NEW, dtype=jnp.int32)[:, None]
    usable = jnp.concatenate([jnp.broadcast_to(cache_live[None, :], (NEW, POOL_COL * PAGE)), causal], axis=1)
    usable = usable[:, None, None, :]
    grouped = q_rot.astype(jnp.float32).reshape(NEW, KVH, group_size, HD)
    scores = jnp.einsum('nkgd,mkd->nkgm', grouped, all_keys) * (1.0 / math.sqrt(HD))
    scores = jnp.where(usable, scores, MASKED)
    highest = lax.optimization_barrier(jnp.max(scores, axis=-1, keepdims=True))
    weights = jnp.where(usable, jnp.exp(scores - highest), 0.0)
    row_total = lax.optimization_barrier(jnp.sum(weights, axis=-1))
    rounded = lax.optimization_barrier(weights.astype(jnp.bfloat16)).astype(jnp.float32)
    blended = jnp.einsum('nkgm,mkd->nkgd', rounded, all_values) / row_total[..., None]
    return blended.reshape(NEW, HQ * HD).astype(jnp.bfloat16)

def expert_layer(moe_rows, expert_ids, gate_probs, w_gate, w_up, w_down):
    slots_all = N_EP * CAP
    flat_ids = expert_ids.reshape(-1)
    flat_probs = jnp.concatenate([gate_probs.reshape(-1), jnp.zeros((1,), gate_probs.dtype)])
    rows_padded = jnp.concatenate([moe_rows, jnp.zeros((1, D), moe_rows.dtype)], axis=0)

    def one_expert(expert):
        entries = jnp.nonzero(flat_ids == expert, size=slots_all, fill_value=MTOK * TOP)[0].astype(jnp.int32)
        tokens = (entries // TOP).astype(jnp.int32)
        picked = rows_padded[tokens]
        gate_full = jnp.transpose(lax.dynamic_slice_in_dim(w_gate, expert * GROUP, GROUP, 0), (1, 0, 2)).reshape(D, FF)
        up_full = jnp.transpose(lax.dynamic_slice_in_dim(w_up, expert * GROUP, GROUP, 0), (1, 0, 2)).reshape(D, FF)
        down_full = lax.dynamic_slice_in_dim(w_down, expert * GROUP, GROUP, 0).reshape(FF, D)
        gate_hid = jnp.dot(picked, gate_full, preferred_element_type=jnp.float32)
        up_hid = jnp.dot(picked, up_full, preferred_element_type=jnp.float32)
        hidden = (jax.nn.silu(gate_hid) * up_hid).astype(jnp.bfloat16)
        expert_val = jnp.dot(hidden, down_full, preferred_element_type=jnp.float32)
        return (expert_val * flat_probs[entries][:, None], tokens)
    outputs, tokens = lax.map(one_expert, jnp.arange(EXPERTS, dtype=jnp.int32))
    summed = jnp.zeros((MTOK + 1, D), jnp.float32).at[tokens.reshape(-1)].add(outputs.reshape(-1, D))
    return summed[:MTOK].astype(jnp.bfloat16)

def reference(queries, new_keys, new_values, cache_keys, cache_values, page_table, cached_len, moe_rows, expert_ids, gate_probs, w_gate, w_up, w_down):
    attn_out = lax.map(lambda bundle: attend_request(*bundle), (queries, new_keys, new_values, cache_keys, cache_values, page_table, cached_len))
    moe_out = expert_layer(moe_rows, expert_ids, gate_probs, w_gate, w_up, w_down)
    return (attn_out, moe_out)
```

```python
import math

import jax
import jax.numpy as jnp
from jax import lax
from jax.sharding import PartitionSpec as P

HD = 128
EXPERTS = 8
TOP = 2
HQ = 16
KVH = 4
PAGE = 128
POOL_DEV = 4
CAP = 16


ROPE_BASE = 10000.0
MASKED = -1e30


def rotary(values, positions):
    half_width = values.shape[-1] // 2
    indices = jnp.arange(half_width, dtype=jnp.float32)
    frequency = jnp.power(ROPE_BASE, -2.0 * indices / values.shape[-1])
    angles = positions.astype(jnp.float32)[:, None] * frequency[None, :]
    cosine = jnp.cos(angles)[:, None, :]
    sine_part = jnp.sin(angles)[:, None, :]
    lower_half = values[..., :half_width]
    upper_half = values[..., half_width:]
    return jnp.concatenate(
        [
            lower_half * cosine - upper_half * sine_part,
            upper_half * cosine + lower_half * sine_part,
        ],
        axis=-1,
    )


def on_device(
    queries,
    new_keys,
    new_values,
    cache_keys,
    cache_values,
    page_table,
    cached_len,
    moe_rows,
    expert_ids,
    gate_probs,
    w_gate,
    w_up,
    w_down,
):
    kv_index = lax.axis_index("kv")
    kv_count = lax.axis_size("kv")
    all_rows = queries.shape[1]
    block_rows = all_rows // kv_count
    length = cached_len[0]
    group_size = HQ // KVH
    score_scale = 1.0 / math.sqrt(HD)
    slot_ids = kv_index * POOL_DEV + jnp.arange(POOL_DEV, dtype=jnp.int32)
    matches = (page_table[0][:, None] == slot_ids[None, :]).astype(jnp.int32)
    page_index = jnp.sum(
        matches * jnp.arange(page_table.shape[1], dtype=jnp.int32)[:, None], axis=0
    )
    cached_pos = (page_index[:, None] * PAGE + jnp.arange(PAGE, dtype=jnp.int32)[None, :]).reshape(
        -1
    )
    block_start = kv_index * block_rows
    own_pos = length + block_start + jnp.arange(block_rows, dtype=jnp.int32)
    key_block = lax.dynamic_slice_in_dim(new_keys[0], block_start, block_rows, 0)
    value_block = lax.dynamic_slice_in_dim(new_values[0], block_start, block_rows, 0)
    own_keys = rotary(key_block.astype(jnp.float32).reshape(block_rows, KVH, HD), own_pos).astype(
        jnp.bfloat16
    )
    local_keys = jnp.concatenate([cache_keys[0].reshape(-1, KVH, HD), own_keys], axis=0)
    local_values = jnp.concatenate(
        [cache_values[0].reshape(-1, KVH, HD), value_block.reshape(block_rows, KVH, HD)], axis=0
    )
    key_pos = jnp.concatenate([cached_pos, own_pos])
    live_keys = jnp.concatenate([cached_pos < length, jnp.ones((block_rows,), jnp.bool_)])
    positions = length + jnp.arange(all_rows, dtype=jnp.int32)
    rotated = rotary(queries[0].astype(jnp.float32).reshape(all_rows, HQ, HD), positions).astype(
        jnp.bfloat16
    )
    grouped = rotated.reshape(all_rows, KVH, group_size, HD)
    scores = (
        jnp.einsum("nkgd,mkd->nkgm", grouped, local_keys, preferred_element_type=jnp.float32)
        * score_scale
    )
    usable = (live_keys[None, :] & (key_pos[None, :] <= positions[:, None]))[:, None, None, :]
    scores = jnp.where(usable, scores, MASKED)
    part_high = jnp.max(scores, axis=-1)
    highest = lax.pmax(part_high, "kv")
    weights = jnp.where(usable, jnp.exp(scores - highest[..., None]), 0.0)
    part_total = jnp.sum(weights, axis=-1)
    part_blend = jnp.einsum(
        "nkgm,mkd->nkgd",
        weights.astype(jnp.bfloat16),
        local_values,
        preferred_element_type=jnp.float32,
    )
    total_row = jnp.pad(part_total.reshape(1, -1), ((0, 0), (0, HQ * HD - all_rows * HQ)))
    packed = lax.psum(
        jnp.concatenate([part_blend.reshape(all_rows, HQ * HD), total_row], axis=0), "kv"
    )
    row_total = packed[all_rows, : all_rows * HQ].reshape(all_rows, HQ)
    blended = packed[:all_rows].reshape(all_rows, HQ, HD)
    attn_out = (
        (blended / row_total[..., None])
        .reshape(1, all_rows, HQ * HD)
        .astype(jnp.bfloat16)
    )
    ep_count = lax.axis_size("ep")
    share_count = ep_count // EXPERTS
    tok_rows = moe_rows.shape[0]
    slot_total = ep_count * CAP
    flat_ids = expert_ids.reshape(-1)
    one_hot = (flat_ids[:, None] == jnp.arange(EXPERTS, dtype=jnp.int32)[None, :]).astype(jnp.int32)
    earlier = jnp.cumsum(one_hot, axis=0) - one_hot
    slot_rank = jnp.sum(earlier * one_hot, axis=1)
    slot_index = jnp.arange(slot_total, dtype=jnp.int32)
    dest_expert = slot_index // CAP // share_count
    dest_slot = slot_index % CAP
    matched = (flat_ids[None, :] == dest_expert[:, None]) & (
        slot_rank[None, :] == dest_slot[:, None]
    )
    select = jnp.sum(matched.astype(jnp.float32).reshape(slot_total, tok_rows, TOP), axis=2).astype(
        jnp.bfloat16
    )
    weight_map = jnp.sum(
        jnp.where(matched, gate_probs.reshape(-1)[None, :], 0.0).reshape(slot_total, tok_rows, TOP),
        axis=2,
    )
    col_width = moe_rows.shape[1] // kv_count
    rows_cols = lax.dynamic_slice_in_dim(moe_rows, kv_index * col_width, col_width, 1)
    outgoing = (
        jnp.dot(select, rows_cols, preferred_element_type=jnp.float32)
        .astype(jnp.bfloat16)
        .reshape(ep_count, CAP, -1)
    )
    arrived_cols = lax.all_to_all(outgoing, "ep", split_axis=0, concat_axis=0, tiled=True).reshape(
        slot_total, -1
    )
    arrived = lax.all_gather(arrived_cols, "kv", axis=1, tiled=True)
    gate_proj = jnp.dot(arrived, w_gate[0], preferred_element_type=jnp.float32)
    up_proj = jnp.dot(arrived, w_up[0], preferred_element_type=jnp.float32)
    hidden = (jax.nn.silu(gate_proj) * up_proj).astype(jnp.bfloat16)
    out_width = w_down.shape[2] // kv_count
    down_split = w_down[0].reshape(w_down.shape[1], kv_count, out_width)
    down_cols = lax.all_to_all(down_split, "kv", split_axis=1, concat_axis=0, tiled=True).reshape(
        -1, out_width
    )
    summed = jnp.dot(
        lax.all_gather(hidden, "kv", axis=1, tiled=True),
        down_cols,
        preferred_element_type=jnp.float32,
    )
    returned = (
        lax.all_to_all(
            summed.reshape(ep_count, CAP, -1).astype(jnp.bfloat16),
            "ep",
            split_axis=0,
            concat_axis=0,
            tiled=True,
        )
        .astype(jnp.float32)
        .reshape(slot_total, -1)
    )
    moe_out = jnp.dot(
        weight_map.T, returned, precision=lax.Precision.HIGHEST, preferred_element_type=jnp.float32
    ).astype(jnp.bfloat16)
    return (attn_out, moe_out)


def solution(mesh):
    return jax.shard_map(
        on_device,
        mesh=mesh,
        in_specs=(
            P("ep", None, None),
            P("ep", None, None),
            P("ep", None, None),
            P("ep", "kv", None, None),
            P("ep", "kv", None, None),
            P("ep", None),
            P("ep"),
            P("ep", None),
            P("ep", None),
            P("ep", None),
            P("ep", None, "kv"),
            P("ep", None, "kv"),
            P("ep", "kv", None),
        ),
        out_specs=(P("ep", None, None), P("ep", "kv")),
        check_vma=False,
    )
```

```python
import math

import jax
import jax.numpy as jnp
from jax import lax
from jax.sharding import PartitionSpec as P

HD = 128
EXPERTS = 8
TOP = 2
HQ = 16
KVH = 4
PAGE = 128
POOL_DEV = 4
CAP = 16


ROPE_BASE = 10000.0
MASKED = -1e30


def rotary(values, positions):
    half_width = values.shape[-1] // 2
    indices = jnp.arange(half_width, dtype=jnp.float32)
    frequency = jnp.power(ROPE_BASE, -2.0 * indices / values.shape[-1])
    angles = positions.astype(jnp.float32)[:, None] * frequency[None, :]
    cosine = jnp.cos(angles)[:, None, :]
    sine_part = jnp.sin(angles)[:, None, :]
    lower_half = values[..., :half_width]
    upper_half = values[..., half_width:]
    return jnp.concatenate(
        [
            lower_half * cosine - upper_half * sine_part,
            upper_half * cosine + lower_half * sine_part,
        ],
        axis=-1,
    )


def on_device(
    queries,
    new_keys,
    new_values,
    cache_keys,
    cache_values,
    page_table,
    cached_len,
    moe_rows,
    expert_ids,
    gate_probs,
    w_gate,
    w_up,
    w_down,
):
    kv_index = lax.axis_index("kv")
    kv_count = lax.axis_size("kv")
    all_rows = queries.shape[1]
    block_rows = all_rows // kv_count
    length = cached_len[0]
    group_size = HQ // KVH
    score_scale = 1.0 / math.sqrt(HD)
    slot_ids = kv_index * POOL_DEV + jnp.arange(POOL_DEV, dtype=jnp.int32)
    matches = (page_table[0][:, None] == slot_ids[None, :]).astype(jnp.int32)
    page_index = jnp.sum(
        matches * jnp.arange(page_table.shape[1], dtype=jnp.int32)[:, None], axis=0
    )
    cached_pos = (page_index[:, None] * PAGE + jnp.arange(PAGE, dtype=jnp.int32)[None, :]).reshape(
        -1
    )
    block_start = kv_index * block_rows
    own_pos = length + block_start + jnp.arange(block_rows, dtype=jnp.int32)
    key_block = lax.dynamic_slice_in_dim(new_keys[0], block_start, block_rows, 0)
    value_block = lax.dynamic_slice_in_dim(new_values[0], block_start, block_rows, 0)
    own_keys = rotary(key_block.astype(jnp.float32).reshape(block_rows, KVH, HD), own_pos).astype(
        jnp.bfloat16
    )
    local_keys = jnp.concatenate([cache_keys[0].reshape(-1, KVH, HD), own_keys], axis=0)
    local_values = jnp.concatenate(
        [cache_values[0].reshape(-1, KVH, HD), value_block.reshape(block_rows, KVH, HD)], axis=0
    )
    key_pos = jnp.concatenate([cached_pos, own_pos])
    live_keys = jnp.concatenate([cached_pos < length, jnp.ones((block_rows,), jnp.bool_)])
    positions = length + jnp.arange(all_rows, dtype=jnp.int32)
    rotated = rotary(queries[0].astype(jnp.float32).reshape(all_rows, HQ, HD), positions).astype(
        jnp.bfloat16
    )
    grouped = rotated.reshape(all_rows, KVH, group_size, HD)
    scores = (
        jnp.einsum("nkgd,mkd->nkgm", grouped, local_keys, preferred_element_type=jnp.float32)
        * score_scale
    )
    usable = (live_keys[None, :] & (key_pos[None, :] <= positions[:, None]))[:, None, None, :]
    scores = jnp.where(usable, scores, MASKED)
    part_high = jnp.max(scores, axis=-1)
    weights = jnp.where(usable, jnp.exp(scores - part_high[..., None]), 0.0)
    part_total = jnp.sum(weights, axis=-1)
    part_blend = jnp.einsum(
        "nkgm,mkd->nkgd",
        weights.astype(jnp.bfloat16),
        local_values,
        preferred_element_type=jnp.float32,
    )
    packed = jnp.concatenate(
        [
            part_blend.reshape(all_rows, HQ * HD),
            part_high.reshape(all_rows, HQ),
            part_total.reshape(all_rows, HQ),
        ],
        axis=1,
    ).reshape(kv_count, block_rows, -1)
    parts = lax.all_to_all(packed, "kv", split_axis=0, concat_axis=0, tiled=True).reshape(
        kv_count, block_rows, -1
    )
    parts_blend = parts[..., : HQ * HD].reshape(kv_count, block_rows, HQ, HD)
    parts_high = parts[..., HQ * HD : HQ * HD + HQ]
    parts_total = parts[..., HQ * HD + HQ :]
    highest = jnp.max(parts_high, axis=0)
    factor = jnp.exp(parts_high - highest[None])
    row_total = jnp.sum(parts_total * factor, axis=0)
    blended = jnp.sum(parts_blend * factor[..., None], axis=0)
    own_out = (blended / row_total[..., None]).reshape(block_rows, HQ * HD).astype(jnp.bfloat16)
    attn_out = lax.all_gather(own_out, "kv", axis=0, tiled=True).reshape(1, all_rows, HQ * HD)
    ep_count = lax.axis_size("ep")
    share_count = ep_count // EXPERTS
    tok_rows = moe_rows.shape[0]
    slot_total = ep_count * CAP
    flat_ids = expert_ids.reshape(-1)
    one_hot = (flat_ids[:, None] == jnp.arange(EXPERTS, dtype=jnp.int32)[None, :]).astype(jnp.int32)
    earlier = jnp.cumsum(one_hot, axis=0) - one_hot
    slot_rank = jnp.sum(earlier * one_hot, axis=1)
    slot_index = jnp.arange(slot_total, dtype=jnp.int32)
    dest_expert = slot_index // CAP // share_count
    dest_slot = slot_index % CAP
    matched = (flat_ids[None, :] == dest_expert[:, None]) & (
        slot_rank[None, :] == dest_slot[:, None]
    )
    select = jnp.sum(matched.astype(jnp.float32).reshape(slot_total, tok_rows, TOP), axis=2).astype(
        jnp.bfloat16
    )
    weight_map = jnp.sum(
        jnp.where(matched, gate_probs.reshape(-1)[None, :], 0.0).reshape(slot_total, tok_rows, TOP),
        axis=2,
    )
    col_width = moe_rows.shape[1] // kv_count
    rows_cols = lax.dynamic_slice_in_dim(moe_rows, kv_index * col_width, col_width, 1)
    outgoing = (
        jnp.dot(select, rows_cols, preferred_element_type=jnp.float32)
        .astype(jnp.bfloat16)
        .reshape(ep_count, CAP, -1)
    )
    arrived_cols = lax.all_to_all(outgoing, "ep", split_axis=0, concat_axis=0, tiled=True).reshape(
        slot_total, -1
    )
    arrived = lax.all_gather(arrived_cols, "kv", axis=1, tiled=True)
    gate_proj = jnp.dot(arrived, w_gate[0], preferred_element_type=jnp.float32)
    up_proj = jnp.dot(arrived, w_up[0], preferred_element_type=jnp.float32)
    hidden = (jax.nn.silu(gate_proj) * up_proj).astype(jnp.bfloat16)
    out_width = w_down.shape[2] // kv_count
    down_split = w_down[0].reshape(w_down.shape[1], kv_count, out_width)
    down_cols = lax.all_to_all(down_split, "kv", split_axis=1, concat_axis=0, tiled=True).reshape(
        -1, out_width
    )
    summed = jnp.dot(
        lax.all_gather(hidden, "kv", axis=1, tiled=True),
        down_cols,
        preferred_element_type=jnp.float32,
    )
    returned = (
        lax.all_to_all(
            summed.reshape(ep_count, CAP, -1).astype(jnp.bfloat16),
            "ep",
            split_axis=0,
            concat_axis=0,
            tiled=True,
        )
        .astype(jnp.float32)
        .reshape(slot_total, -1)
    )
    moe_out = jnp.dot(
        weight_map.T, returned, precision=lax.Precision.HIGHEST, preferred_element_type=jnp.float32
    ).astype(jnp.bfloat16)
    return (attn_out, moe_out)


def solution(mesh):
    return jax.shard_map(
        on_device,
        mesh=mesh,
        in_specs=(
            P("ep", None, None),
            P("ep", None, None),
            P("ep", None, None),
            P("ep", "kv", None, None),
            P("ep", "kv", None, None),
            P("ep", None),
            P("ep"),
            P("ep", None),
            P("ep", None),
            P("ep", None),
            P("ep", None, "kv"),
            P("ep", None, "kv"),
            P("ep", "kv", None),
        ),
        out_specs=(P("ep", None, None), P("ep", "kv")),
        check_vma=False,
    )
```

```python
import math

import jax
import jax.numpy as jnp
from jax import lax
from jax.sharding import PartitionSpec as P

HD = 128
EXPERTS = 8
TOP = 2
HQ = 16
KVH = 4
PAGE = 128
POOL_DEV = 4
CAP = 16


ROPE_BASE = 10000.0
MASKED = -1e30


def rotary(values, positions):
    half_width = values.shape[-1] // 2
    indices = jnp.arange(half_width, dtype=jnp.float32)
    frequency = jnp.power(ROPE_BASE, -2.0 * indices / values.shape[-1])
    angles = positions.astype(jnp.float32)[:, None] * frequency[None, :]
    cosine = jnp.cos(angles)[:, None, :]
    sine_part = jnp.sin(angles)[:, None, :]
    lower_half = values[..., :half_width]
    upper_half = values[..., half_width:]
    return jnp.concatenate(
        [
            lower_half * cosine - upper_half * sine_part,
            upper_half * cosine + lower_half * sine_part,
        ],
        axis=-1,
    )


def on_device(
    queries,
    new_keys,
    new_values,
    cache_keys,
    cache_values,
    page_table,
    cached_len,
    moe_rows,
    expert_ids,
    gate_probs,
    w_gate,
    w_up,
    w_down,
):
    kv_index = lax.axis_index("kv")
    kv_count = lax.axis_size("kv")
    all_rows = queries.shape[1]
    block_rows = all_rows // kv_count
    length = cached_len[0]
    group_size = HQ // KVH
    score_scale = 1.0 / math.sqrt(HD)
    out_width = w_down.shape[2] // kv_count
    down_split = w_down[0].reshape(w_down.shape[1], kv_count, out_width)
    down_cols = lax.all_to_all(down_split, "kv", split_axis=1, concat_axis=0, tiled=True).reshape(
        -1, out_width
    )
    ep_count = lax.axis_size("ep")
    share_count = ep_count // EXPERTS
    tok_rows = moe_rows.shape[0]
    slot_total = ep_count * CAP
    flat_ids = expert_ids.reshape(-1)
    one_hot = (flat_ids[:, None] == jnp.arange(EXPERTS, dtype=jnp.int32)[None, :]).astype(jnp.int32)
    earlier = jnp.cumsum(one_hot, axis=0) - one_hot
    slot_rank = jnp.sum(earlier * one_hot, axis=1)
    slot_index = jnp.arange(slot_total, dtype=jnp.int32)
    dest_expert = slot_index // CAP // share_count
    dest_slot = slot_index % CAP
    matched = (flat_ids[None, :] == dest_expert[:, None]) & (
        slot_rank[None, :] == dest_slot[:, None]
    )
    select = jnp.sum(matched.astype(jnp.float32).reshape(slot_total, tok_rows, TOP), axis=2).astype(
        jnp.bfloat16
    )
    weight_map = jnp.sum(
        jnp.where(matched, gate_probs.reshape(-1)[None, :], 0.0).reshape(slot_total, tok_rows, TOP),
        axis=2,
    )
    col_width = moe_rows.shape[1] // kv_count
    rows_cols = lax.dynamic_slice_in_dim(moe_rows, kv_index * col_width, col_width, 1)
    outgoing = (
        jnp.dot(select, rows_cols, preferred_element_type=jnp.float32)
        .astype(jnp.bfloat16)
        .reshape(ep_count, CAP, -1)
    )
    arrived_cols = lax.all_to_all(outgoing, "ep", split_axis=0, concat_axis=0, tiled=True).reshape(
        slot_total, -1
    )
    arrived = lax.all_gather(arrived_cols, "kv", axis=1, tiled=True)
    arrived_cols, queries, new_keys, new_values, cache_keys, cache_values = lax.optimization_barrier(
        (arrived_cols, queries, new_keys, new_values, cache_keys, cache_values)
    )
    slot_ids = kv_index * POOL_DEV + jnp.arange(POOL_DEV, dtype=jnp.int32)
    matches = (page_table[0][:, None] == slot_ids[None, :]).astype(jnp.int32)
    page_index = jnp.sum(
        matches * jnp.arange(page_table.shape[1], dtype=jnp.int32)[:, None], axis=0
    )
    cached_pos = (page_index[:, None] * PAGE + jnp.arange(PAGE, dtype=jnp.int32)[None, :]).reshape(
        -1
    )
    block_start = kv_index * block_rows
    own_pos = length + block_start + jnp.arange(block_rows, dtype=jnp.int32)
    key_block = lax.dynamic_slice_in_dim(new_keys[0], block_start, block_rows, 0)
    value_block = lax.dynamic_slice_in_dim(new_values[0], block_start, block_rows, 0)
    own_keys = rotary(key_block.astype(jnp.float32).reshape(block_rows, KVH, HD), own_pos).astype(
        jnp.bfloat16
    )
    local_keys = jnp.concatenate([cache_keys[0].reshape(-1, KVH, HD), own_keys], axis=0)
    local_values = jnp.concatenate(
        [cache_values[0].reshape(-1, KVH, HD), value_block.reshape(block_rows, KVH, HD)], axis=0
    )
    key_pos = jnp.concatenate([cached_pos, own_pos])
    live_keys = jnp.concatenate([cached_pos < length, jnp.ones((block_rows,), jnp.bool_)])
    positions = length + jnp.arange(all_rows, dtype=jnp.int32)
    rotated = rotary(queries[0].astype(jnp.float32).reshape(all_rows, HQ, HD), positions).astype(
        jnp.bfloat16
    )
    grouped = rotated.reshape(all_rows, KVH, group_size, HD)
    scores = (
        jnp.einsum("nkgd,mkd->nkgm", grouped, local_keys, preferred_element_type=jnp.float32)
        * score_scale
    )
    usable = (live_keys[None, :] & (key_pos[None, :] <= positions[:, None]))[:, None, None, :]
    scores = jnp.where(usable, scores, MASKED)
    part_high = jnp.max(scores, axis=-1)
    weights = jnp.where(usable, jnp.exp(scores - part_high[..., None]), 0.0)
    part_total = jnp.sum(weights, axis=-1)
    part_blend = jnp.einsum(
        "nkgm,mkd->nkgd",
        weights.astype(jnp.bfloat16),
        local_values,
        preferred_element_type=jnp.float32,
    )
    packed = jnp.concatenate(
        [
            part_blend.reshape(all_rows, HQ * HD),
            part_high.reshape(all_rows, HQ),
            part_total.reshape(all_rows, HQ),
        ],
        axis=1,
    ).reshape(kv_count, block_rows, -1)
    parts = lax.all_to_all(packed, "kv", split_axis=0, concat_axis=0, tiled=True).reshape(
        kv_count, block_rows, -1
    )
    parts_blend = parts[..., : HQ * HD].reshape(kv_count, block_rows, HQ, HD)
    parts_high = parts[..., HQ * HD : HQ * HD + HQ]
    parts_total = parts[..., HQ * HD + HQ :]
    highest = jnp.max(parts_high, axis=0)
    factor = jnp.exp(parts_high - highest[None])
    row_total = jnp.sum(parts_total * factor, axis=0)
    blended = jnp.sum(parts_blend * factor[..., None], axis=0)
    own_out = (blended / row_total[..., None]).reshape(block_rows, HQ * HD).astype(jnp.bfloat16)
    attn_out = lax.all_gather(own_out, "kv", axis=0, tiled=True).reshape(1, all_rows, HQ * HD)
    arrived, attn_out, down_cols = lax.optimization_barrier((arrived, attn_out, down_cols))
    gate_proj = jnp.dot(arrived, w_gate[0], preferred_element_type=jnp.float32)
    up_proj = jnp.dot(arrived, w_up[0], preferred_element_type=jnp.float32)
    hidden = (jax.nn.silu(gate_proj) * up_proj).astype(jnp.bfloat16)
    summed = jnp.dot(
        lax.all_gather(hidden, "kv", axis=1, tiled=True),
        down_cols,
        preferred_element_type=jnp.float32,
    )
    returned = (
        lax.all_to_all(
            summed.reshape(ep_count, CAP, -1).astype(jnp.bfloat16),
            "ep",
            split_axis=0,
            concat_axis=0,
            tiled=True,
        )
        .astype(jnp.float32)
        .reshape(slot_total, -1)
    )
    moe_out = jnp.dot(
        weight_map.T, returned, precision=lax.Precision.HIGHEST, preferred_element_type=jnp.float32
    ).astype(jnp.bfloat16)
    return (attn_out, moe_out)

def solution(mesh):
    return jax.shard_map(
        on_device,
        mesh=mesh,
        in_specs=(
            P("ep", None, None),
            P("ep", None, None),
            P("ep", None, None),
            P("ep", "kv", None, None),
            P("ep", "kv", None, None),
            P("ep", None),
            P("ep"),
            P("ep", None),
            P("ep", None),
            P("ep", None),
            P("ep", None, "kv"),
            P("ep", None, "kv"),
            P("ep", "kv", None),
        ),
        out_specs=(P("ep", None, None), P("ep", "kv")),
        check_vma=False,
    )
```

```python
import math

import jax
import jax.numpy as jnp
from jax import lax
from jax.sharding import PartitionSpec as P

HD = 128
EXPERTS = 8
TOP = 2
HQ = 16
KVH = 4
PAGE = 128
POOL_DEV = 4
CAP = 16


ROPE_BASE = 10000.0
MASKED = -1e30


def rotary(values, positions):
    half_width = values.shape[-1] // 2
    indices = jnp.arange(half_width, dtype=jnp.float32)
    frequency = jnp.power(ROPE_BASE, -2.0 * indices / values.shape[-1])
    angles = positions.astype(jnp.float32)[:, None] * frequency[None, :]
    cosine = jnp.cos(angles)[:, None, :]
    sine_part = jnp.sin(angles)[:, None, :]
    lower_half = values[..., :half_width]
    upper_half = values[..., half_width:]
    return jnp.concatenate(
        [
            lower_half * cosine - upper_half * sine_part,
            upper_half * cosine + lower_half * sine_part,
        ],
        axis=-1,
    )


def on_device(
    queries,
    new_keys,
    new_values,
    cache_keys,
    cache_values,
    page_table,
    cached_len,
    moe_rows,
    expert_ids,
    gate_probs,
    w_gate,
    w_up,
    w_down,
):
    kv_index = lax.axis_index("kv")
    kv_count = lax.axis_size("kv")
    all_rows = queries.shape[1]
    block_rows = all_rows // kv_count
    length = cached_len[0]
    group_size = HQ // KVH
    score_scale = 1.0 / math.sqrt(HD)
    out_width = w_down.shape[2] // kv_count
    down_split = w_down[0].reshape(w_down.shape[1], kv_count, out_width)
    down_cols = lax.all_to_all(down_split, "kv", split_axis=1, concat_axis=0, tiled=True).reshape(
        -1, out_width
    )
    ep_count = lax.axis_size("ep")
    share_count = ep_count // EXPERTS
    tok_rows = moe_rows.shape[0]
    slot_total = ep_count * CAP
    flat_ids = expert_ids.reshape(-1)
    one_hot = (flat_ids[:, None] == jnp.arange(EXPERTS, dtype=jnp.int32)[None, :]).astype(jnp.int32)
    earlier = jnp.cumsum(one_hot, axis=0) - one_hot
    slot_rank = jnp.sum(earlier * one_hot, axis=1)
    slot_index = jnp.arange(slot_total, dtype=jnp.int32)
    dest_expert = slot_index // CAP // share_count
    dest_slot = slot_index % CAP
    matched = (flat_ids[None, :] == dest_expert[:, None]) & (
        slot_rank[None, :] == dest_slot[:, None]
    )
    select = jnp.sum(matched.astype(jnp.float32).reshape(slot_total, tok_rows, TOP), axis=2).astype(
        jnp.bfloat16
    )
    weight_map = jnp.sum(
        jnp.where(matched, gate_probs.reshape(-1)[None, :], 0.0).reshape(slot_total, tok_rows, TOP),
        axis=2,
    )
    col_width = moe_rows.shape[1] // kv_count
    rows_cols = lax.dynamic_slice_in_dim(moe_rows, kv_index * col_width, col_width, 1)
    outgoing = (
        jnp.dot(select, rows_cols, preferred_element_type=jnp.float32)
        .astype(jnp.bfloat16)
        .reshape(ep_count, CAP, -1)
    )
    arrived_cols = lax.all_to_all(outgoing, "ep", split_axis=0, concat_axis=0, tiled=True).reshape(
        slot_total, -1
    )
    arrived = lax.all_gather(arrived_cols, "kv", axis=0, tiled=False)
    arrived_cols, queries, new_keys, new_values, cache_keys, cache_values = lax.optimization_barrier(
        (arrived_cols, queries, new_keys, new_values, cache_keys, cache_values)
    )
    slot_ids = kv_index * POOL_DEV + jnp.arange(POOL_DEV, dtype=jnp.int32)
    matches = (page_table[0][:, None] == slot_ids[None, :]).astype(jnp.int32)
    page_index = jnp.sum(
        matches * jnp.arange(page_table.shape[1], dtype=jnp.int32)[:, None], axis=0
    )
    cached_pos = (page_index[:, None] * PAGE + jnp.arange(PAGE, dtype=jnp.int32)[None, :]).reshape(
        -1
    )
    block_start = kv_index * block_rows
    own_pos = length + block_start + jnp.arange(block_rows, dtype=jnp.int32)
    key_block = lax.dynamic_slice_in_dim(new_keys[0], block_start, block_rows, 0)
    value_block = lax.dynamic_slice_in_dim(new_values[0], block_start, block_rows, 0)
    own_keys = rotary(key_block.astype(jnp.float32).reshape(block_rows, KVH, HD), own_pos).astype(
        jnp.bfloat16
    )
    local_keys = jnp.concatenate([cache_keys[0].reshape(-1, KVH, HD), own_keys], axis=0)
    local_values = jnp.concatenate(
        [cache_values[0].reshape(-1, KVH, HD), value_block.reshape(block_rows, KVH, HD)], axis=0
    )
    key_pos = jnp.concatenate([cached_pos, own_pos])
    live_keys = jnp.concatenate([cached_pos < length, jnp.ones((block_rows,), jnp.bool_)])
    positions = length + jnp.arange(all_rows, dtype=jnp.int32)
    rotated = rotary(queries[0].astype(jnp.float32).reshape(all_rows, HQ, HD), positions).astype(
        jnp.bfloat16
    )
    grouped = rotated.reshape(all_rows, KVH, group_size, HD)
    scores = (
        jnp.einsum("nkgd,mkd->nkgm", grouped, local_keys, preferred_element_type=jnp.float32)
        * score_scale
    )
    usable = (live_keys[None, :] & (key_pos[None, :] <= positions[:, None]))[:, None, None, :]
    scores = jnp.where(usable, scores, MASKED)
    part_high = jnp.max(scores, axis=-1)
    weights = jnp.where(usable, jnp.exp(scores - part_high[..., None]), 0.0)
    part_total = jnp.sum(weights, axis=-1)
    part_blend = jnp.einsum(
        "nkgm,mkd->nkgd",
        weights.astype(jnp.bfloat16),
        local_values,
        preferred_element_type=jnp.float32,
    )
    packed = jnp.concatenate(
        [
            part_blend.reshape(all_rows, HQ * HD),
            part_high.reshape(all_rows, HQ),
            part_total.reshape(all_rows, HQ),
        ],
        axis=1,
    ).reshape(kv_count, block_rows, -1)
    parts = lax.all_to_all(packed, "kv", split_axis=0, concat_axis=0, tiled=True).reshape(
        kv_count, block_rows, -1
    )
    parts_blend = parts[..., : HQ * HD].reshape(kv_count, block_rows, HQ, HD)
    parts_high = parts[..., HQ * HD : HQ * HD + HQ]
    parts_total = parts[..., HQ * HD + HQ :]
    highest = jnp.max(parts_high, axis=0)
    factor = jnp.exp(parts_high - highest[None])
    row_total = jnp.sum(parts_total * factor, axis=0)
    blended = jnp.sum(parts_blend * factor[..., None], axis=0)
    own_out = (blended / row_total[..., None]).reshape(block_rows, HQ * HD).astype(jnp.bfloat16)
    attn_out = lax.all_gather(own_out, "kv", axis=0, tiled=True).reshape(1, all_rows, HQ * HD)
    arrived, attn_out, down_cols = lax.optimization_barrier((arrived, attn_out, down_cols))
    gate_w = w_gate[0].reshape(kv_count, col_width, -1)
    up_w = w_up[0].reshape(kv_count, col_width, -1)
    gate_proj = jnp.einsum("ksc,kch->sh", arrived, gate_w, preferred_element_type=jnp.float32)
    up_proj = jnp.einsum("ksc,kch->sh", arrived, up_w, preferred_element_type=jnp.float32)
    hidden = (jax.nn.silu(gate_proj) * up_proj).astype(jnp.bfloat16)
    summed = jnp.einsum(
        "ksh,khc->sc",
        lax.all_gather(hidden, "kv", axis=0, tiled=False),
        down_cols.reshape(kv_count, -1, out_width),
        preferred_element_type=jnp.float32,
    )
    returned = (
        lax.all_to_all(
            summed.reshape(ep_count, CAP, -1).astype(jnp.bfloat16),
            "ep",
            split_axis=0,
            concat_axis=0,
            tiled=True,
        )
        .astype(jnp.float32)
        .reshape(slot_total, -1)
    )
    moe_out = jnp.dot(
        weight_map.T, returned, precision=lax.Precision.HIGHEST, preferred_element_type=jnp.float32
    ).astype(jnp.bfloat16)
    return (attn_out, moe_out)

def solution(mesh):
    return jax.shard_map(
        on_device,
        mesh=mesh,
        in_specs=(
            P("ep", None, None),
            P("ep", None, None),
            P("ep", None, None),
            P("ep", "kv", None, None),
            P("ep", "kv", None, None),
            P("ep", None),
            P("ep"),
            P("ep", None),
            P("ep", None),
            P("ep", None),
            P("ep", None, "kv"),
            P("ep", None, "kv"),
            P("ep", "kv", None),
        ),
        out_specs=(P("ep", None, None), P("ep", "kv")),
        check_vma=False,
    )
```

```python
import math

import jax
import jax.numpy as jnp
from jax import lax
from jax.sharding import PartitionSpec as P

HD = 128
EXPERTS = 8
TOP = 2
HQ = 16
KVH = 4
PAGE = 128
POOL_DEV = 4
CAP = 16


ROPE_BASE = 10000.0
MASKED = -1e30


def rotary(values, positions):
    half_width = values.shape[-1] // 2
    indices = jnp.arange(half_width, dtype=jnp.float32)
    frequency = jnp.power(ROPE_BASE, -2.0 * indices / values.shape[-1])
    angles = positions.astype(jnp.float32)[:, None] * frequency[None, :]
    cosine = jnp.cos(angles)[:, None, :]
    sine_part = jnp.sin(angles)[:, None, :]
    lower_half = values[..., :half_width]
    upper_half = values[..., half_width:]
    return jnp.concatenate(
        [
            lower_half * cosine - upper_half * sine_part,
            upper_half * cosine + lower_half * sine_part,
        ],
        axis=-1,
    )


def on_device(
    queries,
    new_keys,
    new_values,
    cache_keys,
    cache_values,
    page_table,
    cached_len,
    moe_rows,
    expert_ids,
    gate_probs,
    w_gate,
    w_up,
    w_down,
):
    kv_index = lax.axis_index("kv")
    kv_count = lax.axis_size("kv")
    all_rows = queries.shape[1]
    block_rows = all_rows // kv_count
    length = cached_len[0]
    group_size = HQ // KVH
    score_scale = 1.0 / math.sqrt(HD)
    out_width = w_down.shape[2] // kv_count
    down_split = w_down[0].reshape(w_down.shape[1], kv_count, out_width)
    down_cols = lax.all_to_all(down_split, "kv", split_axis=1, concat_axis=0, tiled=True).reshape(
        -1, out_width
    )
    ep_count = lax.axis_size("ep")
    share_count = ep_count // EXPERTS
    tok_rows = moe_rows.shape[0]
    slot_total = ep_count * CAP
    flat_ids = expert_ids.reshape(-1)
    one_hot = (flat_ids[:, None] == jnp.arange(EXPERTS, dtype=jnp.int32)[None, :]).astype(jnp.int32)
    earlier = jnp.cumsum(one_hot, axis=0) - one_hot
    slot_rank = jnp.sum(earlier * one_hot, axis=1)
    slot_index = jnp.arange(slot_total, dtype=jnp.int32)
    dest_expert = slot_index // CAP // share_count
    dest_slot = slot_index % CAP
    matched = (flat_ids[None, :] == dest_expert[:, None]) & (
        slot_rank[None, :] == dest_slot[:, None]
    )
    select = jnp.sum(matched.astype(jnp.float32).reshape(slot_total, tok_rows, TOP), axis=2).astype(
        jnp.bfloat16
    )
    weight_map = jnp.sum(
        jnp.where(matched, gate_probs.reshape(-1)[None, :], 0.0).reshape(slot_total, tok_rows, TOP),
        axis=2,
    )
    col_width = moe_rows.shape[1] // kv_count
    rows_cols = lax.dynamic_slice_in_dim(moe_rows, kv_index * col_width, col_width, 1)
    outgoing = (
        jnp.dot(select, rows_cols, preferred_element_type=jnp.float32)
        .astype(jnp.bfloat16)
        .reshape(ep_count, CAP, -1)
    )
    arrived_cols = lax.all_to_all(outgoing, "ep", split_axis=0, concat_axis=0, tiled=True).reshape(
        slot_total, -1
    )
    arrived = lax.all_gather(arrived_cols, "kv", axis=0, tiled=False)
    arrived_cols, queries, new_keys, new_values, cache_keys, cache_values = lax.optimization_barrier(
        (arrived_cols, queries, new_keys, new_values, cache_keys, cache_values)
    )
    slot_ids = kv_index * POOL_DEV + jnp.arange(POOL_DEV, dtype=jnp.int32)
    matches = (page_table[0][:, None] == slot_ids[None, :]).astype(jnp.int32)
    page_index = jnp.sum(
        matches * jnp.arange(page_table.shape[1], dtype=jnp.int32)[:, None], axis=0
    )
    cached_pos = (page_index[:, None] * PAGE + jnp.arange(PAGE, dtype=jnp.int32)[None, :]).reshape(
        -1
    )
    block_start = kv_index * block_rows
    own_pos = length + block_start + jnp.arange(block_rows, dtype=jnp.int32)
    key_block = lax.dynamic_slice_in_dim(new_keys[0], block_start, block_rows, 0)
    value_block = lax.dynamic_slice_in_dim(new_values[0], block_start, block_rows, 0)
    own_keys = rotary(key_block.astype(jnp.float32).reshape(block_rows, KVH, HD), own_pos).astype(
        jnp.bfloat16
    )
    local_keys = jnp.concatenate([cache_keys[0].reshape(-1, KVH, HD), own_keys], axis=0)
    local_values = jnp.concatenate(
        [cache_values[0].reshape(-1, KVH, HD), value_block.reshape(block_rows, KVH, HD)], axis=0
    )
    key_pos = jnp.concatenate([cached_pos, own_pos])
    live_keys = jnp.concatenate([cached_pos < length, jnp.ones((block_rows,), jnp.bool_)])
    positions = length + jnp.arange(all_rows, dtype=jnp.int32)
    rotated = rotary(queries[0].astype(jnp.float32).reshape(all_rows, HQ, HD), positions).astype(
        jnp.bfloat16
    )
    grouped = rotated.reshape(all_rows, KVH, group_size, HD)
    scores = (
        jnp.einsum("nkgd,mkd->nkgm", grouped, local_keys, preferred_element_type=jnp.float32)
        * score_scale
    )
    usable = (live_keys[None, :] & (key_pos[None, :] <= positions[:, None]))[:, None, None, :]
    scores = jnp.where(usable, scores, MASKED)
    part_high = jnp.max(scores, axis=-1)
    weights = jnp.where(usable, jnp.exp(scores - part_high[..., None]), 0.0)
    part_total = jnp.sum(weights, axis=-1)
    part_blend = jnp.einsum(
        "nkgm,mkd->nkgd",
        weights.astype(jnp.bfloat16),
        local_values,
        preferred_element_type=jnp.float32,
    )
    packed = jnp.concatenate(
        [
            part_blend.reshape(all_rows, HQ * HD),
            part_high.reshape(all_rows, HQ),
            part_total.reshape(all_rows, HQ),
        ],
        axis=1,
    ).reshape(kv_count, block_rows, -1)
    parts = lax.all_to_all(packed, "kv", split_axis=0, concat_axis=0, tiled=True).reshape(
        kv_count, block_rows, -1
    )
    parts_blend = parts[..., : HQ * HD].reshape(kv_count, block_rows, HQ, HD)
    parts_high = parts[..., HQ * HD : HQ * HD + HQ]
    parts_total = parts[..., HQ * HD + HQ :]
    highest = jnp.max(parts_high, axis=0)
    factor = jnp.exp(parts_high - highest[None])
    row_total = jnp.sum(parts_total * factor, axis=0)
    blended = jnp.sum(parts_blend * factor[..., None], axis=0)
    own_out = (blended / row_total[..., None]).reshape(block_rows, HQ * HD).astype(jnp.bfloat16)
    arrived, own_out, down_cols = lax.optimization_barrier((arrived, own_out, down_cols))
    gate_w = w_gate[0].reshape(kv_count, col_width, -1)
    up_w = w_up[0].reshape(kv_count, col_width, -1)
    gate_proj = jnp.einsum("ksc,kch->sh", arrived, gate_w, preferred_element_type=jnp.float32)
    up_proj = jnp.einsum("ksc,kch->sh", arrived, up_w, preferred_element_type=jnp.float32)
    hidden = (jax.nn.silu(gate_proj) * up_proj).astype(jnp.bfloat16)
    hidden_width = hidden.shape[1]
    joined = lax.all_gather(
        jnp.concatenate([hidden, own_out.reshape(-1, hidden_width)], axis=0), "kv", axis=0, tiled=False
    )
    attn_out = joined[:, slot_total:].reshape(1, all_rows, HQ * HD)
    summed = jnp.einsum(
        "ksh,khc->sc",
        joined[:, :slot_total],
        down_cols.reshape(kv_count, -1, out_width),
        preferred_element_type=jnp.float32,
    )
    returned = (
        lax.all_to_all(
            summed.reshape(ep_count, CAP, -1).astype(jnp.bfloat16),
            "ep",
            split_axis=0,
            concat_axis=0,
            tiled=True,
        )
        .astype(jnp.float32)
        .reshape(slot_total, -1)
    )
    moe_out = jnp.dot(
        weight_map.T, returned, precision=lax.Precision.HIGHEST, preferred_element_type=jnp.float32
    ).astype(jnp.bfloat16)
    return (attn_out, moe_out)

def solution(mesh):
    return jax.shard_map(
        on_device,
        mesh=mesh,
        in_specs=(
            P("ep", None, None),
            P("ep", None, None),
            P("ep", None, None),
            P("ep", "kv", None, None),
            P("ep", "kv", None, None),
            P("ep", None),
            P("ep"),
            P("ep", None),
            P("ep", None),
            P("ep", None),
            P("ep", None, "kv"),
            P("ep", None, "kv"),
            P("ep", "kv", None),
        ),
        out_specs=(P("ep", None, None), P("ep", "kv")),
        check_vma=False,
    )
```

```python
import math

import jax
import jax.numpy as jnp
from jax import lax
from jax.sharding import PartitionSpec as P

HD = 128
EXPERTS = 8
TOP = 2
HQ = 16
KVH = 4
PAGE = 128
POOL_DEV = 4
CAP = 16


ROPE_BASE = 10000.0
MASKED = -1e30


def rotary(values, positions):
    half_width = values.shape[-1] // 2
    indices = jnp.arange(half_width, dtype=jnp.float32)
    frequency = jnp.power(ROPE_BASE, -2.0 * indices / values.shape[-1])
    angles = positions.astype(jnp.float32)[:, None] * frequency[None, :]
    cosine = jnp.cos(angles)[:, None, :]
    sine_part = jnp.sin(angles)[:, None, :]
    lower_half = values[..., :half_width]
    upper_half = values[..., half_width:]
    return jnp.concatenate(
        [
            lower_half * cosine - upper_half * sine_part,
            upper_half * cosine + lower_half * sine_part,
        ],
        axis=-1,
    )


def bf16_pieces(values, count):
    pieces = []
    rest = values
    for _ in range(count):
        rounded = lax.reduce_precision(rest, exponent_bits=8, mantissa_bits=7)
        pieces.append(rounded.astype(jnp.bfloat16))
        rest = rest - rounded
    return jnp.stack(pieces, axis=1)


def from_pieces(pieces):
    total = pieces[:, 0].astype(jnp.float32)
    for index in range(1, pieces.shape[1]):
        total = total + pieces[:, index].astype(jnp.float32)
    return total


def on_device(
    queries,
    new_keys,
    new_values,
    cache_keys,
    cache_values,
    page_table,
    cached_len,
    moe_rows,
    expert_ids,
    gate_probs,
    w_gate,
    w_up,
    w_down,
):
    kv_index = lax.axis_index("kv")
    kv_count = lax.axis_size("kv")
    all_rows = queries.shape[1]
    block_rows = all_rows // kv_count
    length = cached_len[0]
    group_size = HQ // KVH
    score_scale = 1.0 / math.sqrt(HD)
    out_width = w_down.shape[2] // kv_count
    down_split = w_down[0].reshape(w_down.shape[1], kv_count, out_width)
    down_out = jnp.transpose(down_split, (1, 0, 2)).reshape(kv_count, -1)
    ep_count = lax.axis_size("ep")
    share_count = ep_count // EXPERTS
    tok_rows = moe_rows.shape[0]
    slot_total = ep_count * CAP
    flat_ids = expert_ids.reshape(-1)
    one_hot = (flat_ids[:, None] == jnp.arange(EXPERTS, dtype=jnp.int32)[None, :]).astype(jnp.int32)
    earlier = jnp.cumsum(one_hot, axis=0) - one_hot
    slot_rank = jnp.sum(earlier * one_hot, axis=1)
    slot_index = jnp.arange(slot_total, dtype=jnp.int32)
    dest_expert = slot_index // CAP // share_count
    dest_slot = slot_index % CAP
    matched = (flat_ids[None, :] == dest_expert[:, None]) & (
        slot_rank[None, :] == dest_slot[:, None]
    )
    select = jnp.sum(matched.astype(jnp.float32).reshape(slot_total, tok_rows, TOP), axis=2).astype(
        jnp.bfloat16
    )
    weight_map = jnp.sum(
        jnp.where(matched, gate_probs.reshape(-1)[None, :], 0.0).reshape(slot_total, tok_rows, TOP),
        axis=2,
    )
    col_width = moe_rows.shape[1] // kv_count
    rows_cols = lax.dynamic_slice_in_dim(moe_rows, kv_index * col_width, col_width, 1)
    outgoing = (
        jnp.dot(select, rows_cols, preferred_element_type=jnp.float32)
        .astype(jnp.bfloat16)
        .reshape(ep_count, CAP, -1)
    )
    arrived_cols = lax.all_to_all(outgoing, "ep", split_axis=0, concat_axis=0, tiled=True).reshape(
        slot_total, -1
    )
    arrived = lax.all_gather(arrived_cols, "kv", axis=0, tiled=False)
    arrived_cols, queries, new_keys, new_values, cache_keys, cache_values = lax.optimization_barrier(
        (arrived_cols, queries, new_keys, new_values, cache_keys, cache_values)
    )
    slot_ids = kv_index * POOL_DEV + jnp.arange(POOL_DEV, dtype=jnp.int32)
    matches = (page_table[0][:, None] == slot_ids[None, :]).astype(jnp.int32)
    page_index = jnp.sum(
        matches * jnp.arange(page_table.shape[1], dtype=jnp.int32)[:, None], axis=0
    )
    cached_pos = (page_index[:, None] * PAGE + jnp.arange(PAGE, dtype=jnp.int32)[None, :]).reshape(
        -1
    )
    block_start = kv_index * block_rows
    own_pos = length + block_start + jnp.arange(block_rows, dtype=jnp.int32)
    key_block = lax.dynamic_slice_in_dim(new_keys[0], block_start, block_rows, 0)
    value_block = lax.dynamic_slice_in_dim(new_values[0], block_start, block_rows, 0)
    own_keys = rotary(key_block.astype(jnp.float32).reshape(block_rows, KVH, HD), own_pos).astype(
        jnp.bfloat16
    )
    local_keys = jnp.concatenate([cache_keys[0].reshape(-1, KVH, HD), own_keys], axis=0)
    local_values = jnp.concatenate(
        [cache_values[0].reshape(-1, KVH, HD), value_block.reshape(block_rows, KVH, HD)], axis=0
    )
    key_pos = jnp.concatenate([cached_pos, own_pos])
    live_keys = jnp.concatenate([cached_pos < length, jnp.ones((block_rows,), jnp.bool_)])
    positions = length + jnp.arange(all_rows, dtype=jnp.int32)
    rotated = rotary(queries[0].astype(jnp.float32).reshape(all_rows, HQ, HD), positions).astype(
        jnp.bfloat16
    )
    grouped = rotated.reshape(all_rows, KVH, group_size, HD)
    scores = (
        jnp.einsum("nkgd,mkd->nkgm", grouped, local_keys, preferred_element_type=jnp.float32)
        * score_scale
    )
    usable = (live_keys[None, :] & (key_pos[None, :] <= positions[:, None]))[:, None, None, :]
    scores = jnp.where(usable, scores, MASKED)
    part_high = jnp.max(scores, axis=-1)
    weights = jnp.where(usable, jnp.exp(scores - part_high[..., None]), 0.0)
    part_total = jnp.sum(weights, axis=-1)
    part_blend = jnp.einsum(
        "nkgm,mkd->nkgd",
        weights.astype(jnp.bfloat16),
        local_values,
        preferred_element_type=jnp.float32,
    )
    sums_out = jnp.concatenate(
        [part_blend.reshape(all_rows, HQ * HD), part_total.reshape(all_rows, HQ)], axis=1
    ).reshape(kv_count, block_rows, -1)
    high_out = part_high.reshape(kv_count, block_rows, HQ)
    sums_pieces = bf16_pieces(sums_out, 2)
    high_pieces = bf16_pieces(high_out, 3)
    sums_len = 2 * sums_out[0].size
    high_len = 3 * high_out[0].size
    outbound = jnp.concatenate(
        [sums_pieces.reshape(kv_count, -1), high_pieces.reshape(kv_count, -1), down_out], axis=1
    )
    inbound = lax.all_to_all(outbound, "kv", split_axis=0, concat_axis=0, tiled=True)
    parts_sums = from_pieces(inbound[:, :sums_len].reshape((kv_count, 2) + sums_out.shape[1:]))
    parts_high = from_pieces(
        inbound[:, sums_len : sums_len + high_len].reshape((kv_count, 3) + high_out.shape[1:])
    )
    down_cols = inbound[:, sums_len + high_len :].reshape(-1, out_width)
    parts_blend = parts_sums[..., : HQ * HD].reshape(kv_count, block_rows, HQ, HD)
    parts_total = parts_sums[..., HQ * HD :]
    highest = jnp.max(parts_high, axis=0)
    factor = jnp.exp(parts_high - highest[None])
    row_total = jnp.sum(parts_total * factor, axis=0)
    blended = jnp.sum(parts_blend * factor[..., None], axis=0)
    own_out = (blended / row_total[..., None]).reshape(block_rows, HQ * HD).astype(jnp.bfloat16)
    arrived, own_out, down_cols = lax.optimization_barrier((arrived, own_out, down_cols))
    gate_w = w_gate[0].reshape(kv_count, col_width, -1)
    up_w = w_up[0].reshape(kv_count, col_width, -1)
    gate_proj = jnp.einsum("ksc,kch->sh", arrived, gate_w, preferred_element_type=jnp.float32)
    up_proj = jnp.einsum("ksc,kch->sh", arrived, up_w, preferred_element_type=jnp.float32)
    hidden = (jax.nn.silu(gate_proj) * up_proj).astype(jnp.bfloat16)
    hidden_width = hidden.shape[1]
    joined = lax.all_gather(
        jnp.concatenate([hidden, own_out.reshape(-1, hidden_width)], axis=0), "kv", axis=0, tiled=False
    )
    attn_out = joined[:, slot_total:].reshape(1, all_rows, HQ * HD)
    summed = jnp.einsum(
        "ksh,khc->sc",
        joined[:, :slot_total],
        down_cols.reshape(kv_count, -1, out_width),
        preferred_element_type=jnp.float32,
    )
    returned = (
        lax.all_to_all(
            summed.reshape(ep_count, CAP, -1).astype(jnp.bfloat16),
            "ep",
            split_axis=0,
            concat_axis=0,
            tiled=True,
        )
        .astype(jnp.float32)
        .reshape(slot_total, -1)
    )
    moe_out = jnp.dot(
        weight_map.T, returned, precision=lax.Precision.HIGHEST, preferred_element_type=jnp.float32
    ).astype(jnp.bfloat16)
    return (attn_out, moe_out)

def solution(mesh):
    return jax.shard_map(
        on_device,
        mesh=mesh,
        in_specs=(
            P("ep", None, None),
            P("ep", None, None),
            P("ep", None, None),
            P("ep", "kv", None, None),
            P("ep", "kv", None, None),
            P("ep", None),
            P("ep"),
            P("ep", None),
            P("ep", None),
            P("ep", None),
            P("ep", None, "kv"),
            P("ep", None, "kv"),
            P("ep", "kv", None),
        ),
        out_specs=(P("ep", None, None), P("ep", "kv")),
        check_vma=False,
    )
```

```python
import math

import jax
import jax.numpy as jnp
from jax import lax
from jax.sharding import PartitionSpec as P

HD = 128
EXPERTS = 8
TOP = 2
HQ = 16
KVH = 4
PAGE = 128
POOL_DEV = 4
CAP = 16


ROPE_BASE = 10000.0
MASKED = -1e30


def rotary(values, positions):
    half_width = values.shape[-1] // 2
    indices = jnp.arange(half_width, dtype=jnp.float32)
    frequency = jnp.power(ROPE_BASE, -2.0 * indices / values.shape[-1])
    angles = positions.astype(jnp.float32)[:, None] * frequency[None, :]
    cosine = jnp.cos(angles)[:, None, :]
    sine_part = jnp.sin(angles)[:, None, :]
    lower_half = values[..., :half_width]
    upper_half = values[..., half_width:]
    return jnp.concatenate(
        [
            lower_half * cosine - upper_half * sine_part,
            upper_half * cosine + lower_half * sine_part,
        ],
        axis=-1,
    )


def ring_gather(piece, kv_index, kv_count):
    z_count = kv_count // 2
    z_here = kv_index // 2
    core = kv_index % 2
    ahead = [(2 * z + c, 2 * ((z + 1) % z_count) + c) for z in range(z_count) for c in range(2)]
    behind = [(2 * z + c, 2 * ((z - 1) % z_count) + c) for z in range(z_count) for c in range(2)]
    swap = [(2 * z + c, 2 * z + 1 - c) for z in range(z_count) for c in range(2)]
    forward_steps = z_count // 2
    backward_steps = z_count - 1 - forward_steps
    plane = [piece]
    sources = [z_here]
    moving = piece
    for step in range(1, forward_steps + 1):
        moving = lax.ppermute(moving, "kv", ahead)
        plane.append(moving)
        sources.append((z_here - step) % z_count)
    moving = piece
    for step in range(1, backward_steps + 1):
        moving = lax.ppermute(moving, "kv", behind)
        plane.append(moving)
        sources.append((z_here + step) % z_count)
    own_plane = jnp.stack(plane)
    other_plane = lax.ppermute(own_plane, "kv", swap)
    source_z = jnp.stack(sources)
    piece_ids = jnp.concatenate([2 * source_z + core, 2 * source_z + 1 - core])
    return jnp.concatenate([own_plane, other_plane]), piece_ids


def on_device(
    queries,
    new_keys,
    new_values,
    cache_keys,
    cache_values,
    page_table,
    cached_len,
    moe_rows,
    expert_ids,
    gate_probs,
    w_gate,
    w_up,
    w_down,
):
    kv_index = lax.axis_index("kv")
    kv_count = lax.axis_size("kv")
    all_rows = queries.shape[1]
    block_rows = all_rows // kv_count
    length = cached_len[0]
    group_size = HQ // KVH
    score_scale = 1.0 / math.sqrt(HD)
    out_width = w_down.shape[2] // kv_count
    down_split = w_down[0].reshape(w_down.shape[1], kv_count, out_width)
    down_cols = lax.all_to_all(down_split, "kv", split_axis=1, concat_axis=0, tiled=True).reshape(
        -1, out_width
    )
    ep_count = lax.axis_size("ep")
    share_count = ep_count // EXPERTS
    tok_rows = moe_rows.shape[0]
    slot_total = ep_count * CAP
    flat_ids = expert_ids.reshape(-1)
    one_hot = (flat_ids[:, None] == jnp.arange(EXPERTS, dtype=jnp.int32)[None, :]).astype(jnp.int32)
    earlier = jnp.cumsum(one_hot, axis=0) - one_hot
    slot_rank = jnp.sum(earlier * one_hot, axis=1)
    slot_index = jnp.arange(slot_total, dtype=jnp.int32)
    dest_expert = slot_index // CAP // share_count
    dest_slot = slot_index % CAP
    matched = (flat_ids[None, :] == dest_expert[:, None]) & (
        slot_rank[None, :] == dest_slot[:, None]
    )
    select = jnp.sum(matched.astype(jnp.float32).reshape(slot_total, tok_rows, TOP), axis=2).astype(
        jnp.bfloat16
    )
    weight_map = jnp.sum(
        jnp.where(matched, gate_probs.reshape(-1)[None, :], 0.0).reshape(slot_total, tok_rows, TOP),
        axis=2,
    )
    col_width = moe_rows.shape[1] // kv_count
    rows_cols = lax.dynamic_slice_in_dim(moe_rows, kv_index * col_width, col_width, 1)
    outgoing = (
        jnp.dot(select, rows_cols, preferred_element_type=jnp.float32)
        .astype(jnp.bfloat16)
        .reshape(ep_count, CAP, -1)
    )
    arrived_cols = lax.all_to_all(outgoing, "ep", split_axis=0, concat_axis=0, tiled=True).reshape(
        slot_total, -1
    )
    arrived, piece_ids = ring_gather(arrived_cols, kv_index, kv_count)
    arrived_cols, queries, new_keys, new_values, cache_keys, cache_values = lax.optimization_barrier(
        (arrived_cols, queries, new_keys, new_values, cache_keys, cache_values)
    )
    slot_ids = kv_index * POOL_DEV + jnp.arange(POOL_DEV, dtype=jnp.int32)
    matches = (page_table[0][:, None] == slot_ids[None, :]).astype(jnp.int32)
    page_index = jnp.sum(
        matches * jnp.arange(page_table.shape[1], dtype=jnp.int32)[:, None], axis=0
    )
    cached_pos = (page_index[:, None] * PAGE + jnp.arange(PAGE, dtype=jnp.int32)[None, :]).reshape(
        -1
    )
    block_start = kv_index * block_rows
    own_pos = length + block_start + jnp.arange(block_rows, dtype=jnp.int32)
    key_block = lax.dynamic_slice_in_dim(new_keys[0], block_start, block_rows, 0)
    value_block = lax.dynamic_slice_in_dim(new_values[0], block_start, block_rows, 0)
    own_keys = rotary(key_block.astype(jnp.float32).reshape(block_rows, KVH, HD), own_pos).astype(
        jnp.bfloat16
    )
    local_keys = jnp.concatenate([cache_keys[0].reshape(-1, KVH, HD), own_keys], axis=0)
    local_values = jnp.concatenate(
        [cache_values[0].reshape(-1, KVH, HD), value_block.reshape(block_rows, KVH, HD)], axis=0
    )
    key_pos = jnp.concatenate([cached_pos, own_pos])
    live_keys = jnp.concatenate([cached_pos < length, jnp.ones((block_rows,), jnp.bool_)])
    positions = length + jnp.arange(all_rows, dtype=jnp.int32)
    rotated = rotary(queries[0].astype(jnp.float32).reshape(all_rows, HQ, HD), positions).astype(
        jnp.bfloat16
    )
    grouped = rotated.reshape(all_rows, KVH, group_size, HD)
    scores = (
        jnp.einsum("nkgd,mkd->nkgm", grouped, local_keys, preferred_element_type=jnp.float32)
        * score_scale
    )
    usable = (live_keys[None, :] & (key_pos[None, :] <= positions[:, None]))[:, None, None, :]
    scores = jnp.where(usable, scores, MASKED)
    part_high = jnp.max(scores, axis=-1)
    weights = jnp.where(usable, jnp.exp(scores - part_high[..., None]), 0.0)
    part_total = jnp.sum(weights, axis=-1)
    part_blend = jnp.einsum(
        "nkgm,mkd->nkgd",
        weights.astype(jnp.bfloat16),
        local_values,
        preferred_element_type=jnp.float32,
    )
    packed = jnp.concatenate(
        [
            part_blend.reshape(all_rows, HQ * HD),
            part_high.reshape(all_rows, HQ),
            part_total.reshape(all_rows, HQ),
        ],
        axis=1,
    ).reshape(kv_count, block_rows, -1)
    parts = lax.all_to_all(packed, "kv", split_axis=0, concat_axis=0, tiled=True).reshape(
        kv_count, block_rows, -1
    )
    parts_blend = parts[..., : HQ * HD].reshape(kv_count, block_rows, HQ, HD)
    parts_high = parts[..., HQ * HD : HQ * HD + HQ]
    parts_total = parts[..., HQ * HD + HQ :]
    highest = jnp.max(parts_high, axis=0)
    factor = jnp.exp(parts_high - highest[None])
    row_total = jnp.sum(parts_total * factor, axis=0)
    blended = jnp.sum(parts_blend * factor[..., None], axis=0)
    own_out = (blended / row_total[..., None]).reshape(block_rows, HQ * HD).astype(jnp.bfloat16)
    arrived, own_out, down_cols = lax.optimization_barrier((arrived, own_out, down_cols))
    gate_w = w_gate[0].reshape(kv_count, col_width, -1)[piece_ids]
    up_w = w_up[0].reshape(kv_count, col_width, -1)[piece_ids]
    gate_proj = jnp.einsum("ksc,kch->sh", arrived, gate_w, preferred_element_type=jnp.float32)
    up_proj = jnp.einsum("ksc,kch->sh", arrived, up_w, preferred_element_type=jnp.float32)
    hidden = (jax.nn.silu(gate_proj) * up_proj).astype(jnp.bfloat16)
    hidden_width = hidden.shape[1]
    joined = lax.all_gather(
        jnp.concatenate([hidden, own_out.reshape(-1, hidden_width)], axis=0), "kv", axis=0, tiled=False
    )
    attn_out = joined[:, slot_total:].reshape(1, all_rows, HQ * HD)
    summed = jnp.einsum(
        "ksh,khc->sc",
        joined[:, :slot_total],
        down_cols.reshape(kv_count, -1, out_width),
        preferred_element_type=jnp.float32,
    )
    returned = (
        lax.all_to_all(
            summed.reshape(ep_count, CAP, -1).astype(jnp.bfloat16),
            "ep",
            split_axis=0,
            concat_axis=0,
            tiled=True,
        )
        .astype(jnp.float32)
        .reshape(slot_total, -1)
    )
    moe_out = jnp.dot(
        weight_map.T, returned, precision=lax.Precision.HIGHEST, preferred_element_type=jnp.float32
    ).astype(jnp.bfloat16)
    return (attn_out, moe_out)

def solution(mesh):
    return jax.shard_map(
        on_device,
        mesh=mesh,
        in_specs=(
            P("ep", None, None),
            P("ep", None, None),
            P("ep", None, None),
            P("ep", "kv", None, None),
            P("ep", "kv", None, None),
            P("ep", None),
            P("ep"),
            P("ep", None),
            P("ep", None),
            P("ep", None),
            P("ep", None, "kv"),
            P("ep", None, "kv"),
            P("ep", "kv", None),
        ),
        out_specs=(P("ep", None, None), P("ep", "kv")),
        check_vma=False,
    )
```

```python
import math

import jax
import jax.numpy as jnp
from jax import lax
from jax.sharding import PartitionSpec as P

HD = 128
EXPERTS = 8
TOP = 2
HQ = 16
KVH = 4
PAGE = 128
POOL_DEV = 4
CAP = 16


ROPE_BASE = 10000.0
MASKED = -1e30


def rotary(values, positions):
    half_width = values.shape[-1] // 2
    indices = jnp.arange(half_width, dtype=jnp.float32)
    frequency = jnp.power(ROPE_BASE, -2.0 * indices / values.shape[-1])
    angles = positions.astype(jnp.float32)[:, None] * frequency[None, :]
    cosine = jnp.cos(angles)[:, None, :]
    sine_part = jnp.sin(angles)[:, None, :]
    lower_half = values[..., :half_width]
    upper_half = values[..., half_width:]
    return jnp.concatenate(
        [
            lower_half * cosine - upper_half * sine_part,
            upper_half * cosine + lower_half * sine_part,
        ],
        axis=-1,
    )


def on_device(
    queries,
    new_keys,
    new_values,
    cache_keys,
    cache_values,
    page_table,
    cached_len,
    moe_rows,
    expert_ids,
    gate_probs,
    w_gate,
    w_up,
    w_down,
):
    kv_index = lax.axis_index("kv")
    kv_count = lax.axis_size("kv")
    all_rows = queries.shape[1]
    block_rows = all_rows // kv_count
    length = cached_len[0]
    group_size = HQ // KVH
    score_scale = 1.0 / math.sqrt(HD)
    out_width = w_down.shape[2] // kv_count
    down_split = w_down[0].reshape(w_down.shape[1], kv_count, out_width)
    down_cols = lax.all_to_all(down_split, "kv", split_axis=1, concat_axis=0, tiled=True).reshape(
        -1, out_width
    )
    ep_count = lax.axis_size("ep")
    share_count = ep_count // EXPERTS
    tok_rows = moe_rows.shape[0]
    slot_total = ep_count * CAP
    flat_ids = expert_ids.reshape(-1)
    one_hot = (flat_ids[:, None] == jnp.arange(EXPERTS, dtype=jnp.int32)[None, :]).astype(jnp.int32)
    earlier = jnp.cumsum(one_hot, axis=0) - one_hot
    slot_rank = jnp.sum(earlier * one_hot, axis=1)
    slot_index = jnp.arange(slot_total, dtype=jnp.int32)
    dest_expert = slot_index // CAP // share_count
    dest_slot = slot_index % CAP
    matched = (flat_ids[None, :] == dest_expert[:, None]) & (
        slot_rank[None, :] == dest_slot[:, None]
    )
    select = jnp.sum(matched.astype(jnp.float32).reshape(slot_total, tok_rows, TOP), axis=2).astype(
        jnp.bfloat16
    )
    weight_map = jnp.sum(
        jnp.where(matched, gate_probs.reshape(-1)[None, :], 0.0).reshape(slot_total, tok_rows, TOP),
        axis=2,
    )
    col_width = moe_rows.shape[1] // kv_count
    rows_cols = lax.dynamic_slice_in_dim(moe_rows, kv_index * col_width, col_width, 1)
    outgoing = (
        jnp.dot(select, rows_cols, preferred_element_type=jnp.float32)
        .astype(jnp.bfloat16)
        .reshape(ep_count, CAP, -1)
    )
    arrived_cols = lax.all_to_all(outgoing, "ep", split_axis=0, concat_axis=0, tiled=True).reshape(
        slot_total, -1
    )
    arrived = lax.all_gather(arrived_cols, "kv", axis=0, tiled=False)
    arrived_cols, down_cols, queries, new_keys, new_values, cache_keys, cache_values = (
        lax.optimization_barrier(
            (arrived_cols, down_cols, queries, new_keys, new_values, cache_keys, cache_values)
        )
    )
    slot_ids = kv_index * POOL_DEV + jnp.arange(POOL_DEV, dtype=jnp.int32)
    matches = (page_table[0][:, None] == slot_ids[None, :]).astype(jnp.int32)
    page_index = jnp.sum(
        matches * jnp.arange(page_table.shape[1], dtype=jnp.int32)[:, None], axis=0
    )
    cached_pos = (page_index[:, None] * PAGE + jnp.arange(PAGE, dtype=jnp.int32)[None, :]).reshape(
        -1
    )
    block_start = kv_index * block_rows
    own_pos = length + block_start + jnp.arange(block_rows, dtype=jnp.int32)
    key_block = lax.dynamic_slice_in_dim(new_keys[0], block_start, block_rows, 0)
    value_block = lax.dynamic_slice_in_dim(new_values[0], block_start, block_rows, 0)
    own_keys = rotary(key_block.astype(jnp.float32).reshape(block_rows, KVH, HD), own_pos).astype(
        jnp.bfloat16
    )
    local_keys = jnp.concatenate([cache_keys[0].reshape(-1, KVH, HD), own_keys], axis=0)
    local_values = jnp.concatenate(
        [cache_values[0].reshape(-1, KVH, HD), value_block.reshape(block_rows, KVH, HD)], axis=0
    )
    key_pos = jnp.concatenate([cached_pos, own_pos])
    live_keys = jnp.concatenate([cached_pos < length, jnp.ones((block_rows,), jnp.bool_)])
    positions = length + jnp.arange(all_rows, dtype=jnp.int32)
    rotated = rotary(queries[0].astype(jnp.float32).reshape(all_rows, HQ, HD), positions).astype(
        jnp.bfloat16
    )
    grouped = rotated.reshape(all_rows, KVH, group_size, HD)
    scores = (
        jnp.einsum("nkgd,mkd->nkgm", grouped, local_keys, preferred_element_type=jnp.float32)
        * score_scale
    )
    usable = (live_keys[None, :] & (key_pos[None, :] <= positions[:, None]))[:, None, None, :]
    scores = jnp.where(usable, scores, MASKED)
    part_high = jnp.max(scores, axis=-1)
    weights = jnp.where(usable, jnp.exp(scores - part_high[..., None]), 0.0)
    part_total = jnp.sum(weights, axis=-1)
    part_blend = jnp.einsum(
        "nkgm,mkd->nkgd",
        weights.astype(jnp.bfloat16),
        local_values,
        preferred_element_type=jnp.float32,
    )
    packed = jnp.concatenate(
        [
            part_blend.reshape(all_rows, HQ * HD),
            part_high.reshape(all_rows, HQ),
            part_total.reshape(all_rows, HQ),
        ],
        axis=1,
    ).reshape(kv_count, block_rows, -1)
    parts = lax.all_to_all(packed, "kv", split_axis=0, concat_axis=0, tiled=True).reshape(
        kv_count, block_rows, -1
    )
    parts_blend = parts[..., : HQ * HD].reshape(kv_count, block_rows, HQ, HD)
    parts_high = parts[..., HQ * HD : HQ * HD + HQ]
    parts_total = parts[..., HQ * HD + HQ :]
    highest = jnp.max(parts_high, axis=0)
    factor = jnp.exp(parts_high - highest[None])
    row_total = jnp.sum(parts_total * factor, axis=0)
    blended = jnp.sum(parts_blend * factor[..., None], axis=0)
    own_out = (blended / row_total[..., None]).reshape(block_rows, HQ * HD).astype(jnp.bfloat16)
    arrived, own_out, down_cols = lax.optimization_barrier((arrived, own_out, down_cols))
    gate_w = w_gate[0].reshape(kv_count, col_width, -1)
    up_w = w_up[0].reshape(kv_count, col_width, -1)
    gate_proj = jnp.einsum("ksc,kch->sh", arrived, gate_w, preferred_element_type=jnp.float32)
    up_proj = jnp.einsum("ksc,kch->sh", arrived, up_w, preferred_element_type=jnp.float32)
    hidden = (jax.nn.silu(gate_proj) * up_proj).astype(jnp.bfloat16)
    hidden_width = hidden.shape[1]
    joined = lax.all_gather(
        jnp.concatenate([hidden, own_out.reshape(-1, hidden_width)], axis=0), "kv", axis=0, tiled=False
    )
    attn_out = joined[:, slot_total:].reshape(1, all_rows, HQ * HD)
    summed = jnp.einsum(
        "ksh,khc->sc",
        joined[:, :slot_total],
        down_cols.reshape(kv_count, -1, out_width),
        preferred_element_type=jnp.float32,
    )
    returned = (
        lax.all_to_all(
            summed.reshape(ep_count, CAP, -1).astype(jnp.bfloat16),
            "ep",
            split_axis=0,
            concat_axis=0,
            tiled=True,
        )
        .astype(jnp.float32)
        .reshape(slot_total, -1)
    )
    moe_out = jnp.dot(
        weight_map.T, returned, precision=lax.Precision.HIGHEST, preferred_element_type=jnp.float32
    ).astype(jnp.bfloat16)
    return (attn_out, moe_out)

def solution(mesh):
    return jax.shard_map(
        on_device,
        mesh=mesh,
        in_specs=(
            P("ep", None, None),
            P("ep", None, None),
            P("ep", None, None),
            P("ep", "kv", None, None),
            P("ep", "kv", None, None),
            P("ep", None),
            P("ep"),
            P("ep", None),
            P("ep", None),
            P("ep", None),
            P("ep", None, "kv"),
            P("ep", None, "kv"),
            P("ep", "kv", None),
        ),
        out_specs=(P("ep", None, None), P("ep", "kv")),
        check_vma=False,
    )
```

```python
import math

import jax
import jax.numpy as jnp
from jax import lax
from jax.sharding import PartitionSpec as P

HD = 128
EXPERTS = 8
TOP = 2
HQ = 16
KVH = 4
PAGE = 128
POOL_DEV = 4
CAP = 16


ROPE_BASE = 10000.0
MASKED = -1e30


def rotary(values, positions):
    half_width = values.shape[-1] // 2
    indices = jnp.arange(half_width, dtype=jnp.float32)
    frequency = jnp.power(ROPE_BASE, -2.0 * indices / values.shape[-1])
    angles = positions.astype(jnp.float32)[:, None] * frequency[None, :]
    cosine = jnp.cos(angles)[:, None, :]
    sine_part = jnp.sin(angles)[:, None, :]
    lower_half = values[..., :half_width]
    upper_half = values[..., half_width:]
    return jnp.concatenate(
        [
            lower_half * cosine - upper_half * sine_part,
            upper_half * cosine + lower_half * sine_part,
        ],
        axis=-1,
    )


def bf16_pieces(values, count):
    pieces = []
    rest = values
    for _ in range(count):
        rounded = lax.reduce_precision(rest, exponent_bits=8, mantissa_bits=7)
        pieces.append(rounded.astype(jnp.bfloat16))
        rest = rest - rounded
    return jnp.concatenate(pieces, axis=-1)


def from_pieces(pieces):
    total = pieces[:, 0].astype(jnp.float32)
    for index in range(1, pieces.shape[1]):
        total = total + pieces[:, index].astype(jnp.float32)
    return total


def on_device(
    queries,
    new_keys,
    new_values,
    cache_keys,
    cache_values,
    page_table,
    cached_len,
    moe_rows,
    expert_ids,
    gate_probs,
    w_gate,
    w_up,
    w_down,
):
    kv_index = lax.axis_index("kv")
    kv_count = lax.axis_size("kv")
    all_rows = queries.shape[1]
    block_rows = all_rows // kv_count
    length = cached_len[0]
    group_size = HQ // KVH
    score_scale = 1.0 / math.sqrt(HD)
    out_width = w_down.shape[2] // kv_count
    down_split = w_down[0].reshape(w_down.shape[1], kv_count, out_width)
    down_cols = lax.all_to_all(down_split, "kv", split_axis=1, concat_axis=0, tiled=True).reshape(
        -1, out_width
    )
    ep_count = lax.axis_size("ep")
    share_count = ep_count // EXPERTS
    tok_rows = moe_rows.shape[0]
    slot_total = ep_count * CAP
    flat_ids = expert_ids.reshape(-1)
    one_hot = (flat_ids[:, None] == jnp.arange(EXPERTS, dtype=jnp.int32)[None, :]).astype(jnp.int32)
    earlier = jnp.cumsum(one_hot, axis=0) - one_hot
    slot_rank = jnp.sum(earlier * one_hot, axis=1)
    slot_index = jnp.arange(slot_total, dtype=jnp.int32)
    dest_expert = slot_index // CAP // share_count
    dest_slot = slot_index % CAP
    matched = (flat_ids[None, :] == dest_expert[:, None]) & (
        slot_rank[None, :] == dest_slot[:, None]
    )
    select = jnp.sum(matched.astype(jnp.float32).reshape(slot_total, tok_rows, TOP), axis=2).astype(
        jnp.bfloat16
    )
    weight_map = jnp.sum(
        jnp.where(matched, gate_probs.reshape(-1)[None, :], 0.0).reshape(slot_total, tok_rows, TOP),
        axis=2,
    )
    col_width = moe_rows.shape[1] // kv_count
    rows_cols = lax.dynamic_slice_in_dim(moe_rows, kv_index * col_width, col_width, 1)
    outgoing = (
        jnp.dot(select, rows_cols, preferred_element_type=jnp.float32)
        .astype(jnp.bfloat16)
        .reshape(ep_count, CAP, -1)
    )
    arrived_cols = lax.all_to_all(outgoing, "ep", split_axis=0, concat_axis=0, tiled=True).reshape(
        slot_total, -1
    )
    arrived = lax.all_gather(arrived_cols, "kv", axis=0, tiled=False)
    arrived_cols, queries, new_keys, new_values, cache_keys, cache_values = lax.optimization_barrier(
        (arrived_cols, queries, new_keys, new_values, cache_keys, cache_values)
    )
    slot_ids = kv_index * POOL_DEV + jnp.arange(POOL_DEV, dtype=jnp.int32)
    matches = (page_table[0][:, None] == slot_ids[None, :]).astype(jnp.int32)
    page_index = jnp.sum(
        matches * jnp.arange(page_table.shape[1], dtype=jnp.int32)[:, None], axis=0
    )
    cached_pos = (page_index[:, None] * PAGE + jnp.arange(PAGE, dtype=jnp.int32)[None, :]).reshape(
        -1
    )
    block_start = kv_index * block_rows
    own_pos = length + block_start + jnp.arange(block_rows, dtype=jnp.int32)
    key_block = lax.dynamic_slice_in_dim(new_keys[0], block_start, block_rows, 0)
    value_block = lax.dynamic_slice_in_dim(new_values[0], block_start, block_rows, 0)
    own_keys = rotary(key_block.astype(jnp.float32).reshape(block_rows, KVH, HD), own_pos).astype(
        jnp.bfloat16
    )
    local_keys = jnp.concatenate([cache_keys[0].reshape(-1, KVH, HD), own_keys], axis=0)
    local_values = jnp.concatenate(
        [cache_values[0].reshape(-1, KVH, HD), value_block.reshape(block_rows, KVH, HD)], axis=0
    )
    key_pos = jnp.concatenate([cached_pos, own_pos])
    live_keys = jnp.concatenate([cached_pos < length, jnp.ones((block_rows,), jnp.bool_)])
    positions = length + jnp.arange(all_rows, dtype=jnp.int32)
    rotated = rotary(queries[0].astype(jnp.float32).reshape(all_rows, HQ, HD), positions).astype(
        jnp.bfloat16
    )
    grouped = rotated.reshape(all_rows, KVH, group_size, HD)
    scores = (
        jnp.einsum("nkgd,mkd->nkgm", grouped, local_keys, preferred_element_type=jnp.float32)
        * score_scale
    )
    usable = (live_keys[None, :] & (key_pos[None, :] <= positions[:, None]))[:, None, None, :]
    scores = jnp.where(usable, scores, MASKED)
    part_high = jnp.max(scores, axis=-1)
    weights = jnp.where(usable, jnp.exp(scores - part_high[..., None]), 0.0)
    part_total = jnp.sum(weights, axis=-1)
    part_blend = jnp.einsum(
        "nkgm,mkd->nkgd",
        weights.astype(jnp.bfloat16),
        local_values,
        preferred_element_type=jnp.float32,
    )
    small = jnp.concatenate(
        [part_high.reshape(all_rows, HQ), part_total.reshape(all_rows, HQ)], axis=1
    )
    small_pieces = bf16_pieces(small, 3)
    packed = jnp.concatenate(
        [part_blend.reshape(all_rows, HQ * HD).astype(jnp.bfloat16), small_pieces], axis=1
    ).reshape(kv_count, block_rows, -1)
    parts = lax.all_to_all(packed, "kv", split_axis=0, concat_axis=0, tiled=True).reshape(
        kv_count, block_rows, -1
    )
    parts_blend = parts[..., : HQ * HD].astype(jnp.float32).reshape(kv_count, block_rows, HQ, HD)
    parts_small = from_pieces(parts[..., HQ * HD :].reshape(kv_count * block_rows, 3, 2 * HQ))
    parts_small = parts_small.reshape(kv_count, block_rows, 2 * HQ)
    parts_high = parts_small[..., :HQ]
    parts_total = parts_small[..., HQ:]
    highest = jnp.max(parts_high, axis=0)
    factor = jnp.exp(parts_high - highest[None])
    row_total = jnp.sum(parts_total * factor, axis=0)
    blended = jnp.sum(parts_blend * factor[..., None], axis=0)
    own_out = (blended / row_total[..., None]).reshape(block_rows, HQ * HD).astype(jnp.bfloat16)
    arrived, own_out, down_cols = lax.optimization_barrier((arrived, own_out, down_cols))
    gate_w = w_gate[0].reshape(kv_count, col_width, -1)
    up_w = w_up[0].reshape(kv_count, col_width, -1)
    gate_proj = jnp.einsum("ksc,kch->sh", arrived, gate_w, preferred_element_type=jnp.float32)
    up_proj = jnp.einsum("ksc,kch->sh", arrived, up_w, preferred_element_type=jnp.float32)
    hidden = (jax.nn.silu(gate_proj) * up_proj).astype(jnp.bfloat16)
    hidden_width = hidden.shape[1]
    joined = lax.all_gather(
        jnp.concatenate([hidden, own_out.reshape(-1, hidden_width)], axis=0), "kv", axis=0, tiled=False
    )
    attn_out = joined[:, slot_total:].reshape(1, all_rows, HQ * HD)
    summed = jnp.einsum(
        "ksh,khc->sc",
        joined[:, :slot_total],
        down_cols.reshape(kv_count, -1, out_width),
        preferred_element_type=jnp.float32,
    )
    returned = (
        lax.all_to_all(
            summed.reshape(ep_count, CAP, -1).astype(jnp.bfloat16),
            "ep",
            split_axis=0,
            concat_axis=0,
            tiled=True,
        )
        .astype(jnp.float32)
        .reshape(slot_total, -1)
    )
    moe_out = jnp.dot(
        weight_map.T, returned, precision=lax.Precision.HIGHEST, preferred_element_type=jnp.float32
    ).astype(jnp.bfloat16)
    return (attn_out, moe_out)

def solution(mesh):
    return jax.shard_map(
        on_device,
        mesh=mesh,
        in_specs=(
            P("ep", None, None),
            P("ep", None, None),
            P("ep", None, None),
            P("ep", "kv", None, None),
            P("ep", "kv", None, None),
            P("ep", None),
            P("ep"),
            P("ep", None),
            P("ep", None),
            P("ep", None),
            P("ep", None, "kv"),
            P("ep", None, "kv"),
            P("ep", "kv", None),
        ),
        out_specs=(P("ep", None, None), P("ep", "kv")),
        check_vma=False,
    )
```

```python
import math

import jax
import jax.numpy as jnp
from jax import lax
from jax.sharding import PartitionSpec as P

HD = 128
EXPERTS = 8
TOP = 2
HQ = 16
KVH = 4
PAGE = 128
POOL_DEV = 4
CAP = 16


ROPE_BASE = 10000.0
MASKED = -1e30


def rotary(values, positions):
    half_width = values.shape[-1] // 2
    indices = jnp.arange(half_width, dtype=jnp.float32)
    frequency = jnp.power(ROPE_BASE, -2.0 * indices / values.shape[-1])
    angles = positions.astype(jnp.float32)[:, None] * frequency[None, :]
    cosine = jnp.cos(angles)[:, None, :]
    sine_part = jnp.sin(angles)[:, None, :]
    lower_half = values[..., :half_width]
    upper_half = values[..., half_width:]
    return jnp.concatenate(
        [
            lower_half * cosine - upper_half * sine_part,
            upper_half * cosine + lower_half * sine_part,
        ],
        axis=-1,
    )


def bf16_pieces(values, count):
    pieces = []
    rest = values
    for _ in range(count):
        rounded = lax.reduce_precision(rest, exponent_bits=8, mantissa_bits=7)
        pieces.append(rounded.astype(jnp.bfloat16))
        rest = rest - rounded
    return jnp.concatenate(pieces, axis=-1)


def from_pieces(pieces):
    total = pieces[:, 0].astype(jnp.float32)
    for index in range(1, pieces.shape[1]):
        total = total + pieces[:, index].astype(jnp.float32)
    return total


def on_device(
    queries,
    new_keys,
    new_values,
    cache_keys,
    cache_values,
    page_table,
    cached_len,
    moe_rows,
    expert_ids,
    gate_probs,
    w_gate,
    w_up,
    w_down,
):
    kv_index = lax.axis_index("kv")
    kv_count = lax.axis_size("kv")
    all_rows = queries.shape[1]
    block_rows = all_rows // kv_count
    length = cached_len[0]
    group_size = HQ // KVH
    score_scale = 1.0 / math.sqrt(HD)
    out_width = w_down.shape[2] // kv_count
    down_split = w_down[0].reshape(w_down.shape[1], kv_count, out_width)
    down_cols = lax.all_to_all(down_split, "kv", split_axis=1, concat_axis=0, tiled=True).reshape(
        -1, out_width
    )
    ep_count = lax.axis_size("ep")
    share_count = ep_count // EXPERTS
    tok_rows = moe_rows.shape[0]
    slot_total = ep_count * CAP
    flat_ids = expert_ids.reshape(-1)
    one_hot = (flat_ids[:, None] == jnp.arange(EXPERTS, dtype=jnp.int32)[None, :]).astype(jnp.int32)
    earlier = jnp.cumsum(one_hot, axis=0) - one_hot
    slot_rank = jnp.sum(earlier * one_hot, axis=1)
    slot_index = jnp.arange(slot_total, dtype=jnp.int32)
    dest_expert = slot_index // CAP // share_count
    dest_slot = slot_index % CAP
    matched = (flat_ids[None, :] == dest_expert[:, None]) & (
        slot_rank[None, :] == dest_slot[:, None]
    )
    select = jnp.sum(matched.astype(jnp.float32).reshape(slot_total, tok_rows, TOP), axis=2).astype(
        jnp.bfloat16
    )
    weight_map = jnp.sum(
        jnp.where(matched, gate_probs.reshape(-1)[None, :], 0.0).reshape(slot_total, tok_rows, TOP),
        axis=2,
    )
    col_width = moe_rows.shape[1] // kv_count
    rows_cols = lax.dynamic_slice_in_dim(moe_rows, kv_index * col_width, col_width, 1)
    outgoing = (
        jnp.dot(select, rows_cols, preferred_element_type=jnp.float32)
        .astype(jnp.bfloat16)
        .reshape(ep_count, CAP, -1)
    )
    arrived_cols = lax.all_to_all(outgoing, "ep", split_axis=0, concat_axis=0, tiled=True).reshape(
        slot_total, -1
    )
    arrived = lax.all_gather(arrived_cols, "kv", axis=0, tiled=False)
    arrived_cols, queries, new_keys, new_values, cache_keys, cache_values = lax.optimization_barrier(
        (arrived_cols, queries, new_keys, new_values, cache_keys, cache_values)
    )
    slot_ids = kv_index * POOL_DEV + jnp.arange(POOL_DEV, dtype=jnp.int32)
    matches = (page_table[0][:, None] == slot_ids[None, :]).astype(jnp.int32)
    page_index = jnp.sum(
        matches * jnp.arange(page_table.shape[1], dtype=jnp.int32)[:, None], axis=0
    )
    cached_pos = (page_index[:, None] * PAGE + jnp.arange(PAGE, dtype=jnp.int32)[None, :]).reshape(
        -1
    )
    block_start = kv_index * block_rows
    own_pos = length + block_start + jnp.arange(block_rows, dtype=jnp.int32)
    key_block = lax.dynamic_slice_in_dim(new_keys[0], block_start, block_rows, 0)
    value_block = lax.dynamic_slice_in_dim(new_values[0], block_start, block_rows, 0)
    own_keys = rotary(key_block.astype(jnp.float32).reshape(block_rows, KVH, HD), own_pos).astype(
        jnp.bfloat16
    )
    local_keys = jnp.concatenate([cache_keys[0].reshape(-1, KVH, HD), own_keys], axis=0)
    local_values = jnp.concatenate(
        [cache_values[0].reshape(-1, KVH, HD), value_block.reshape(block_rows, KVH, HD)], axis=0
    )
    key_pos = jnp.concatenate([cached_pos, own_pos])
    live_keys = jnp.concatenate([cached_pos < length, jnp.ones((block_rows,), jnp.bool_)])
    positions = length + jnp.arange(all_rows, dtype=jnp.int32)
    rotated = rotary(queries[0].astype(jnp.float32).reshape(all_rows, HQ, HD), positions).astype(
        jnp.bfloat16
    )
    grouped = rotated.reshape(all_rows, KVH, group_size, HD)
    scores = (
        jnp.einsum("nkgd,mkd->nkgm", grouped, local_keys, preferred_element_type=jnp.float32)
        * score_scale
    )
    usable = (live_keys[None, :] & (key_pos[None, :] <= positions[:, None]))[:, None, None, :]
    scores = jnp.where(usable, scores, MASKED)
    part_high = jnp.max(scores, axis=-1)
    weights = jnp.where(usable, jnp.exp(scores - part_high[..., None]), 0.0)
    part_total = jnp.sum(weights, axis=-1)
    part_blend = jnp.einsum(
        "nkgm,mkd->nkgd",
        weights.astype(jnp.bfloat16),
        local_values,
        preferred_element_type=jnp.float32,
    )
    small = jnp.concatenate(
        [part_high.reshape(all_rows, HQ), part_total.reshape(all_rows, HQ)], axis=1
    )
    small_pieces = bf16_pieces(small, 3)
    packed = jnp.concatenate(
        [part_blend.reshape(all_rows, HQ * HD).astype(jnp.bfloat16), small_pieces], axis=1
    ).reshape(kv_count, block_rows, -1)
    parts = lax.all_to_all(packed, "kv", split_axis=0, concat_axis=0, tiled=True).reshape(
        kv_count, block_rows, -1
    )
    parts_blend = parts[..., : HQ * HD].astype(jnp.float32).reshape(kv_count, block_rows, HQ, HD)
    parts_small = from_pieces(parts[..., HQ * HD :].reshape(kv_count * block_rows, 3, 2 * HQ))
    parts_small = parts_small.reshape(kv_count, block_rows, 2 * HQ)
    parts_high = parts_small[..., :HQ]
    parts_total = parts_small[..., HQ:]
    highest = jnp.max(parts_high, axis=0)
    factor = jnp.exp(parts_high - highest[None])
    row_total = jnp.sum(parts_total * factor, axis=0)
    blended = jnp.sum(parts_blend * factor[..., None], axis=0)
    own_out = (blended / row_total[..., None]).reshape(block_rows, HQ * HD).astype(jnp.bfloat16)
    arrived, own_out = lax.optimization_barrier((arrived, own_out))
    gate_w = w_gate[0].reshape(kv_count, col_width, -1)
    up_w = w_up[0].reshape(kv_count, col_width, -1)
    gate_proj = jnp.einsum("ksc,kch->sh", arrived, gate_w, preferred_element_type=jnp.float32)
    up_proj = jnp.einsum("ksc,kch->sh", arrived, up_w, preferred_element_type=jnp.float32)
    hidden = (jax.nn.silu(gate_proj) * up_proj).astype(jnp.bfloat16)
    hidden_width = hidden.shape[1]
    joined = lax.all_gather(
        jnp.concatenate([hidden, own_out.reshape(-1, hidden_width)], axis=0), "kv", axis=0, tiled=False
    )
    attn_out = joined[:, slot_total:].reshape(1, all_rows, HQ * HD)
    summed = jnp.einsum(
        "ksh,khc->sc",
        joined[:, :slot_total],
        down_cols.reshape(kv_count, -1, out_width),
        preferred_element_type=jnp.float32,
    )
    returned = (
        lax.all_to_all(
            summed.reshape(ep_count, CAP, -1).astype(jnp.bfloat16),
            "ep",
            split_axis=0,
            concat_axis=0,
            tiled=True,
        )
        .astype(jnp.float32)
        .reshape(slot_total, -1)
    )
    moe_out = jnp.dot(
        weight_map.T, returned, precision=lax.Precision.HIGHEST, preferred_element_type=jnp.float32
    ).astype(jnp.bfloat16)
    return (attn_out, moe_out)

def solution(mesh):
    return jax.shard_map(
        on_device,
        mesh=mesh,
        in_specs=(
            P("ep", None, None),
            P("ep", None, None),
            P("ep", None, None),
            P("ep", "kv", None, None),
            P("ep", "kv", None, None),
            P("ep", None),
            P("ep"),
            P("ep", None),
            P("ep", None),
            P("ep", None),
            P("ep", None, "kv"),
            P("ep", None, "kv"),
            P("ep", "kv", None),
        ),
        out_specs=(P("ep", None, None), P("ep", "kv")),
        check_vma=False,
    )
```

```python
import math

import jax
import jax.numpy as jnp
from jax import lax
from jax.sharding import PartitionSpec as P

HD = 128
EXPERTS = 8
TOP = 2
HQ = 16
KVH = 4
PAGE = 128
POOL_DEV = 4
CAP = 16


ROPE_BASE = 10000.0
MASKED = -1e30


def rotary(values, positions):
    half_width = values.shape[-1] // 2
    indices = jnp.arange(half_width, dtype=jnp.float32)
    frequency = jnp.power(ROPE_BASE, -2.0 * indices / values.shape[-1])
    angles = positions.astype(jnp.float32)[:, None] * frequency[None, :]
    cosine = jnp.cos(angles)[:, None, :]
    sine_part = jnp.sin(angles)[:, None, :]
    lower_half = values[..., :half_width]
    upper_half = values[..., half_width:]
    return jnp.concatenate(
        [
            lower_half * cosine - upper_half * sine_part,
            upper_half * cosine + lower_half * sine_part,
        ],
        axis=-1,
    )


def bf16_pieces(values, count):
    pieces = []
    rest = values
    for _ in range(count):
        rounded = lax.reduce_precision(rest, exponent_bits=8, mantissa_bits=7)
        pieces.append(rounded.astype(jnp.bfloat16))
        rest = rest - rounded
    return jnp.concatenate(pieces, axis=-1)


def from_pieces(pieces):
    total = pieces[:, 0].astype(jnp.float32)
    for index in range(1, pieces.shape[1]):
        total = total + pieces[:, index].astype(jnp.float32)
    return total


def on_device(
    queries,
    new_keys,
    new_values,
    cache_keys,
    cache_values,
    page_table,
    cached_len,
    moe_rows,
    expert_ids,
    gate_probs,
    w_gate,
    w_up,
    w_down,
):
    kv_index = lax.axis_index("kv")
    kv_count = lax.axis_size("kv")
    all_rows = queries.shape[1]
    block_rows = all_rows // kv_count
    length = cached_len[0]
    group_size = HQ // KVH
    score_scale = 1.0 / math.sqrt(HD)
    out_width = w_down.shape[2] // kv_count
    down_split = w_down[0].reshape(w_down.shape[1], kv_count, out_width)
    down_cols = lax.all_to_all(down_split, "kv", split_axis=1, concat_axis=0, tiled=True).reshape(
        -1, out_width
    )
    ep_count = lax.axis_size("ep")
    share_count = ep_count // EXPERTS
    tok_rows = moe_rows.shape[0]
    slot_total = ep_count * CAP
    flat_ids = expert_ids.reshape(-1)
    one_hot = (flat_ids[:, None] == jnp.arange(EXPERTS, dtype=jnp.int32)[None, :]).astype(jnp.int32)
    earlier = jnp.cumsum(one_hot, axis=0) - one_hot
    slot_rank = jnp.sum(earlier * one_hot, axis=1)
    slot_index = jnp.arange(slot_total, dtype=jnp.int32)
    dest_expert = slot_index // CAP // share_count
    dest_slot = slot_index % CAP
    matched = (flat_ids[None, :] == dest_expert[:, None]) & (
        slot_rank[None, :] == dest_slot[:, None]
    )
    select = jnp.sum(matched.astype(jnp.float32).reshape(slot_total, tok_rows, TOP), axis=2).astype(
        jnp.bfloat16
    )
    weight_map = jnp.sum(
        jnp.where(matched, gate_probs.reshape(-1)[None, :], 0.0).reshape(slot_total, tok_rows, TOP),
        axis=2,
    )
    col_width = moe_rows.shape[1] // kv_count
    rows_cols = lax.dynamic_slice_in_dim(moe_rows, kv_index * col_width, col_width, 1)
    outgoing = (
        jnp.dot(select, rows_cols, preferred_element_type=jnp.float32)
        .astype(jnp.bfloat16)
        .reshape(ep_count, CAP, -1)
    )
    arrived_cols = lax.all_to_all(outgoing, "ep", split_axis=0, concat_axis=0, tiled=True).reshape(
        slot_total, -1
    )
    arrived = lax.all_gather(arrived_cols, "kv", axis=0, tiled=False)
    arrived_cols, queries, new_keys, new_values, cache_keys, cache_values = lax.optimization_barrier(
        (arrived_cols, queries, new_keys, new_values, cache_keys, cache_values)
    )
    slot_ids = kv_index * POOL_DEV + jnp.arange(POOL_DEV, dtype=jnp.int32)
    matches = (page_table[0][:, None] == slot_ids[None, :]).astype(jnp.int32)
    page_index = jnp.sum(
        matches * jnp.arange(page_table.shape[1], dtype=jnp.int32)[:, None], axis=0
    )
    cached_pos = (page_index[:, None] * PAGE + jnp.arange(PAGE, dtype=jnp.int32)[None, :]).reshape(
        -1
    )
    block_start = kv_index * block_rows
    own_pos = length + block_start + jnp.arange(block_rows, dtype=jnp.int32)
    key_block = lax.dynamic_slice_in_dim(new_keys[0], block_start, block_rows, 0)
    value_block = lax.dynamic_slice_in_dim(new_values[0], block_start, block_rows, 0)
    own_keys = rotary(key_block.astype(jnp.float32).reshape(block_rows, KVH, HD), own_pos).astype(
        jnp.bfloat16
    )
    local_keys = jnp.concatenate([cache_keys[0].reshape(-1, KVH, HD), own_keys], axis=0)
    local_values = jnp.concatenate(
        [cache_values[0].reshape(-1, KVH, HD), value_block.reshape(block_rows, KVH, HD)], axis=0
    )
    key_pos = jnp.concatenate([cached_pos, own_pos])
    live_keys = jnp.concatenate([cached_pos < length, jnp.ones((block_rows,), jnp.bool_)])
    positions = length + jnp.arange(all_rows, dtype=jnp.int32)
    rotated = rotary(queries[0].astype(jnp.float32).reshape(all_rows, HQ, HD), positions).astype(
        jnp.bfloat16
    )
    grouped = rotated.reshape(all_rows, KVH, group_size, HD)
    scores = (
        jnp.einsum("nkgd,mkd->nkgm", grouped, local_keys, preferred_element_type=jnp.float32)
        * score_scale
    )
    usable = (live_keys[None, :] & (key_pos[None, :] <= positions[:, None]))[:, None, None, :]
    scores = jnp.where(usable, scores, MASKED)
    part_high = jnp.max(scores, axis=-1)
    weights = jnp.where(usable, jnp.exp(scores - part_high[..., None]), 0.0)
    part_total = jnp.sum(weights, axis=-1)
    part_blend = jnp.einsum(
        "nkgm,mkd->nkgd",
        weights.astype(jnp.bfloat16),
        local_values,
        preferred_element_type=jnp.float32,
    )
    small = jnp.concatenate(
        [part_high.reshape(all_rows, HQ), part_total.reshape(all_rows, HQ)], axis=1
    )
    small_pieces = bf16_pieces(small, 3)
    packed = jnp.concatenate(
        [part_blend.reshape(all_rows, HQ * HD).astype(jnp.bfloat16), small_pieces], axis=1
    ).reshape(kv_count, block_rows, -1)
    parts = lax.all_to_all(packed, "kv", split_axis=0, concat_axis=0, tiled=True).reshape(
        kv_count, block_rows, -1
    )
    parts_blend = parts[..., : HQ * HD].astype(jnp.float32).reshape(kv_count, block_rows, HQ, HD)
    parts_small = from_pieces(parts[..., HQ * HD :].reshape(kv_count * block_rows, 3, 2 * HQ))
    parts_small = parts_small.reshape(kv_count, block_rows, 2 * HQ)
    parts_high = parts_small[..., :HQ]
    parts_total = parts_small[..., HQ:]
    highest = jnp.max(parts_high, axis=0)
    factor = jnp.exp(parts_high - highest[None])
    row_total = jnp.sum(parts_total * factor, axis=0)
    blended = jnp.sum(parts_blend * factor[..., None], axis=0)
    own_out = (blended / row_total[..., None]).reshape(block_rows, HQ * HD).astype(jnp.bfloat16)
    arrived, own_out = lax.optimization_barrier((arrived, own_out))
    gate_w = w_gate[0].reshape(kv_count, col_width, -1)
    up_w = w_up[0].reshape(kv_count, col_width, -1)
    gate_proj = jnp.einsum("ksc,kch->sh", arrived, gate_w, preferred_element_type=jnp.float32)
    up_proj = jnp.einsum("ksc,kch->sh", arrived, up_w, preferred_element_type=jnp.float32)
    hidden = (jax.nn.silu(gate_proj) * up_proj).astype(jnp.bfloat16)
    hidden_width = hidden.shape[1]
    half_cap = CAP // 2
    by_rank = hidden.reshape(ep_count, CAP, hidden_width)
    half_slots = ep_count * half_cap
    down_blocks = down_cols.reshape(kv_count, -1, out_width)
    first = lax.all_gather(
        jnp.concatenate(
            [by_rank[:, :half_cap].reshape(half_slots, hidden_width), own_out.reshape(-1, hidden_width)],
            axis=0,
        ),
        "kv",
        axis=0,
        tiled=False,
    )
    second = lax.all_gather(
        by_rank[:, half_cap:].reshape(half_slots, hidden_width), "kv", axis=0, tiled=False
    )
    attn_out = first[:, half_slots:].reshape(1, all_rows, HQ * HD)

    def project_back(gathered):
        summed = jnp.einsum(
            "ksh,khc->sc", gathered, down_blocks, preferred_element_type=jnp.float32
        )
        return lax.all_to_all(
            summed.reshape(ep_count, half_cap, -1).astype(jnp.bfloat16),
            "ep",
            split_axis=0,
            concat_axis=0,
            tiled=True,
        )

    returned = (
        jnp.concatenate([project_back(first[:, :half_slots]), project_back(second)], axis=1)
        .astype(jnp.float32)
        .reshape(slot_total, -1)
    )
    moe_out = jnp.dot(
        weight_map.T, returned, precision=lax.Precision.HIGHEST, preferred_element_type=jnp.float32
    ).astype(jnp.bfloat16)
    return (attn_out, moe_out)

def solution(mesh):
    return jax.shard_map(
        on_device,
        mesh=mesh,
        in_specs=(
            P("ep", None, None),
            P("ep", None, None),
            P("ep", None, None),
            P("ep", "kv", None, None),
            P("ep", "kv", None, None),
            P("ep", None),
            P("ep"),
            P("ep", None),
            P("ep", None),
            P("ep", None),
            P("ep", None, "kv"),
            P("ep", None, "kv"),
            P("ep", "kv", None),
        ),
        out_specs=(P("ep", None, None), P("ep", "kv")),
        check_vma=False,
    )
```
